256 devices in a mesh: segment: 4 (over x), dp: 64 (over z, y, core).
Axes of the slice: x: 4, y: 4, z: 8, core: 2. Of those that a mesh axis runs over, the one named last changes fastest.
Arguments:
- x_saved: bfloat16 [4, 8192, 1536], P('segment', 'dp'), may hold values from -6 to 6
- gains: float32 [4, 1536], P('segment'), may hold values from 0.1 to 1.9
- w_in: bfloat16 [4, 1536, 3072], P('segment', 'dp'), may hold values from -0.15625 to 0.15625
- w_out: bfloat16 [4, 3072, 1536], P('segment', None, 'dp'), may hold values from -0.109375 to 0.109375
- cotangent: bfloat16 [8192, 1536], P('dp'), may hold values from -6 to 6
- lengths: int32 [64], replicated, may hold values from 1 to 256, 8192 in all
Outputs:
- grads: bfloat16 [4, 8192, 1536], P('segment', 'dp')
- gain_grads: float32 [4, 1536], P('segment')
The draws below stay inside these ranges and needn't reach their ends.
All inputs are finite; a program needn't handle non-finite values.
Results may differ from the reference program's by a relative error of at most 0.0075.
Values may be sent and summed in bfloat16 or wider, within the bound.
No kernel may reach another device: no remote copies, remote signals or barrier semaphores. Data moves between devices by JAX's collectives and lax.ppermute only.
A program may use at most 128 MiB of HBM per device.

```python
import math
import jax
import jax.numpy as jnp
import numpy as np
from jax import lax

D = 1536
FF = 3072
TOK_DEV = 128
TOKENS = 8192
UTTS = 64
MAXLEN = 256
N_SEGMENT = 4


def steps_of(stream_key, dims, pieces, low, largest):
    factor_of, own = 1.0, jax.random.fold_in(stream_key, 6)
    for dim, blocks in pieces:
        draws = jnp.exp(jax.random.uniform(jax.random.fold_in(own, dim), (blocks,), jnp.float32, low / len(pieces), largest / len(pieces)))
        factor_of = factor_of * jnp.repeat(draws, dims[dim] // blocks).reshape([-1 if axis == dim else 1 for axis in range(len(dims))])
    return factor_of


def length_profile(amount, total, bound, skew):
    portions = [(1 << 20) // math.isqrt(grade ** skew) + 1 for grade in range(2, amount + 1)]
    surplus, given = total - bound - (amount - 1), [1] * (amount - 1)
    while surplus > 0:
        free = [i for i in range(amount - 1) if given[i] < bound]
        whole, left = sum([portions[i] for i in free]), surplus
        for i in free:
            extra = min(bound - given[i], max(1, left * portions[i] // whole), surplus)
            given[i] = given[i] + extra
            surplus = surplus - extra
    return np.array([bound] + given)


def ragged(stream_key, count, total, limit, slope):
    if count == 2:
        one = jax.random.randint(stream_key, (), max(1, total - limit), min(limit, total - 1) + 1)
        return jnp.stack([one, total - one])
    tallies = jnp.asarray(length_profile(count, total, limit, slope), jnp.int32)
    twos = (count - 1) // 2
    source_of, taker = tallies[1:1 + 2 * twos:2], tallies[2:2 + 2 * twos:2]
    slack = jnp.minimum(source_of - 1, limit - taker)
    shifted = jax.random.randint(jax.random.fold_in(stream_key, 1), (twos,), 0, 1 << 20) % (slack + 1)
    tallies = tallies.at[1:1 + 2 * twos:2].set(source_of - shifted).at[2:2 + 2 * twos:2].set(taker + shifted)
    return tallies[jax.random.permutation(jax.random.fold_in(stream_key, 2), count)]


def noise(key, dims, deviation, reach, pieces=(), kind=jnp.bfloat16):
    gain = steps_of(key, dims, pieces, -0.22, 0.18) if pieces else 1.0
    values = jax.random.normal(key, dims, jnp.float32) * deviation * gain
    return jnp.minimum(jnp.maximum(values, -reach), reach).astype(kind)


def setup_inputs(seed: int = 0) -> dict:
    key_of = jax.random.split(jax.random.key(seed), 7)
    return {
        "x_saved": noise(key_of[0], (N_SEGMENT, TOKENS, D), 1.0, 6.0, ((0, 4), (1, 64))),
        "gains": jnp.clip(1.0 + 0.18 * jax.random.normal(key_of[1], (N_SEGMENT, D), jnp.float32), 0.1, 1.9),
        "w_in": noise(key_of[2], (N_SEGMENT, D, FF), D ** -0.5, 0.15625, ((0, 4), (1, 64))),
        "w_out": noise(key_of[3], (N_SEGMENT, FF, D), FF ** -0.5, 0.109375, ((0, 4), (2, 64))),
        "cotangent": noise(key_of[4], (TOKENS, D), 1.0, 6.0, ((0, 64),)),
        "lengths": ragged(key_of[5], UTTS, TOKENS, MAXLEN, 2).astype(jnp.int32),
    }


def segment_back(x, gain_vector, w_first, w_second, grad_in):
    xf = x.astype(jnp.float32)
    centered_input = xf - lax.optimization_barrier(jnp.mean(xf, -1, keepdims=True))
    variance = lax.optimization_barrier(jnp.mean(centered_input * centered_input, -1, keepdims=True))
    inverse_deviation = lax.rsqrt(variance + 1e-05)
    standardized_input = centered_input * inverse_deviation
    normalized_input = (standardized_input * gain_vector).astype(jnp.bfloat16)
    hidden = jnp.dot(normalized_input, w_first, preferred_element_type=jnp.float32)
    up_grad = jnp.dot(grad_in, w_second.T, preferred_element_type=jnp.float32)
    sig = jax.nn.sigmoid(hidden)
    hid_grad = (0.5 * up_grad * (sig + hidden * sig * (1.0 - sig))).astype(jnp.bfloat16)
    norm_gradient = jnp.dot(hid_grad, w_first.T, preferred_element_type=jnp.float32)
    gain_partial = lax.optimization_barrier(jnp.sum(norm_gradient * standardized_input, 0))
    gain_scaled = norm_gradient * gain_vector
    backward_result = inverse_deviation * (gain_scaled - lax.optimization_barrier(jnp.mean(gain_scaled, -1, keepdims=True)) - standardized_input * lax.optimization_barrier(jnp.mean(gain_scaled * standardized_input, -1, keepdims=True)))
    return ((grad_in.astype(jnp.float32) + backward_result).astype(jnp.bfloat16), gain_partial)

def reference(x_saved, gains, w_in, w_out, cotangent, lengths):
    ends = jnp.cumsum(lengths)
    position = jnp.arange(TOKENS, dtype=jnp.int32)
    utter = lax.optimization_barrier(jnp.sum((position[:, None] >= ends[None, :]).astype(jnp.int32), 1))
    tok_len = jnp.take(lengths, utter).astype(jnp.float32)
    weight = 2.0 * TOK_DEV / (tok_len + TOK_DEV)
    current = (cotangent.astype(jnp.float32) * weight[:, None]).astype(jnp.bfloat16)
    grad_list = []
    gain_list = []
    for level in range(N_SEGMENT - 1, -1, -1):
        current, gain_partial = segment_back(x_saved[level], gains[level], w_in[level], w_out[level], current)
        grad_list.insert(0, current)
        gain_list.insert(0, gain_partial)
    return (jnp.stack(grad_list), jnp.stack(gain_list))
```

```python
import jax
import jax.numpy as jnp
from jax import lax
import numpy as np
from jax.sharding import Mesh, PartitionSpec as P

DP = ("z", "y", "core")


def passed_along(x, axis, by):
    length = lax.axis_size(axis)
    pairs = [(i, i + by) for i in range(length) if 0 <= i + by < length]
    return lax.ppermute(x, axis, pairs)


def on_device(x_saved, gains, w_in, w_out, cotangent, lengths):
    rows = cotangent.shape[0]
    width = cotangent.shape[1]
    ends = jnp.cumsum(lengths)
    position = lax.axis_index(DP) * rows + jnp.arange(rows, dtype=jnp.int32)
    utter_hit = (position[:, None] >= ends[None, :]).astype(jnp.int32)
    utter = jnp.sum(utter_hit, 1)
    onehot = (utter[:, None] == jnp.arange(lengths.shape[0], dtype=jnp.int32)[None, :]).astype(
        jnp.int32
    )
    tok_len = jnp.sum(onehot * lengths[None, :], 1).astype(jnp.float32)
    weight = 2.0 * rows / (tok_len + rows)
    current = (cotangent.astype(jnp.float32) * weight[:, None]).astype(jnp.bfloat16)
    xf = x_saved[0].astype(jnp.float32)
    centered_input = xf - jnp.mean(xf, -1, keepdims=True)
    variance = jnp.mean(centered_input * centered_input, -1, keepdims=True)
    inverse_deviation = lax.rsqrt(variance + 1e-05)
    standardized_input = centered_input * inverse_deviation
    gain_vector = gains[0]
    normalized_input = (standardized_input * gain_vector).astype(jnp.bfloat16)
    w_first, w_second = (
        lax.all_gather(w_in[0], DP, axis=0, tiled=True),
        lax.all_gather(w_out[0], DP, axis=1, tiled=True),
    )

    def project_all(normed_rows, grad_in):
        hidden = jnp.dot(normed_rows, w_first, preferred_element_type=jnp.float32)
        up_grad = jnp.dot(grad_in, w_second.T, preferred_element_type=jnp.float32)
        sig = jax.nn.sigmoid(hidden)
        hid_grad = (0.5 * up_grad * (sig + hidden * sig * (1.0 - sig))).astype(jnp.bfloat16)
        return jnp.dot(hid_grad, w_first.T, preferred_element_type=jnp.float32)

    def block_back():

        def run(grad_in):
            norm_gradient = project_all(normalized_input, grad_in)
            gain_partial = jnp.sum(norm_gradient * standardized_input, 0)
            gain_scaled = norm_gradient * gain_vector
            backward_result = inverse_deviation * (
                gain_scaled
                - jnp.mean(gain_scaled, -1, keepdims=True)
                - standardized_input * jnp.mean(gain_scaled * standardized_input, -1, keepdims=True)
            )
            return (
                (grad_in.astype(jnp.float32) + backward_result).astype(jnp.bfloat16),
                gain_partial,
            )

        return run

    def pass_through(grad_in):
        return (grad_in, jnp.zeros((width,), jnp.float32))

    segments = lax.axis_size("segment")
    my_segment = lax.axis_index("segment")
    gain_local = jnp.zeros((width,), jnp.float32)
    result = current
    for level in range(segments - 1, -1, -1):
        mine = my_segment == level
        updated, gain_partial = lax.cond(mine, block_back(), pass_through, current)
        result = jnp.where(mine, updated, result)
        gain_local = jnp.where(mine, gain_partial, gain_local)
        if level > 0:
            current = passed_along(updated, "segment", -1)
    gain_total = lax.psum(lax.psum(lax.psum(gain_local, "core"), "y"), "z")
    return (result[None], gain_total[None])


def solution(mesh):
    n_seg, n_dp = mesh.devices.shape
    sizes = dict(zip(("z", "y", "core"), (n_dp // 8, 4, 2)))
    mesh = Mesh(np.asarray(mesh.devices).reshape(n_seg, sizes["z"], sizes["y"], sizes["core"]), ("segment",) + DP)
    in_specs = (
        P("segment", DP, None),
        P("segment", None),
        P("segment", DP, None),
        P("segment", None, DP),
        P(DP, None),
        P(),
    )
    out_specs = (P("segment", DP, None), P("segment", None))
    return jax.shard_map(
        on_device, mesh=mesh, in_specs=in_specs, out_specs=out_specs, check_vma=False
    )
```

```python
import jax
import jax.numpy as jnp
import numpy as np
from jax import lax
from jax.experimental import pallas as pl
from jax.experimental.pallas import tpu as pltpu
from jax.sharding import Mesh, PartitionSpec as P

DP = ("z", "y", "core")
CHUNK = 512


def segment_kernel(z_ref, g_ref, xh_ref, inv_ref, gain_ref, w1_ref, w2_ref, out_ref, gp_ref, acc_ref):
    k = pl.program_id(0)

    @pl.when(k == 0)
    def _():
        acc_ref[...] = jnp.zeros_like(acc_ref)

    w1 = w1_ref[...]
    hidden = jnp.dot(z_ref[...], w1, preferred_element_type=jnp.float32)
    up_grad = jnp.dot(g_ref[...], w2_ref[...], preferred_element_type=jnp.float32)
    sig = jax.nn.sigmoid(hidden)
    hid_grad = (0.5 * up_grad * (sig + hidden * sig * (1.0 - sig))).astype(jnp.bfloat16)
    acc_ref[...] += lax.dot_general(
        hid_grad, w1, (((1,), (1,)), ((), ())), preferred_element_type=jnp.float32
    )

    @pl.when(k == pl.num_programs(0) - 1)
    def _():
        norm_gradient = acc_ref[...]
        standardized = xh_ref[...]
        gp_ref[...] = jnp.sum(norm_gradient * standardized, axis=0, keepdims=True)
        gain_scaled = norm_gradient * gain_ref[...]
        mean_e = jnp.mean(gain_scaled, axis=-1, keepdims=True)
        mean_ex = jnp.mean(gain_scaled * standardized, axis=-1, keepdims=True)
        back = inv_ref[...] * (gain_scaled - mean_e - standardized * mean_ex)
        out_ref[...] = (g_ref[...].astype(jnp.float32) + back).astype(out_ref.dtype)


def segment_back(normed, grad_in, standardized, inverse_deviation, gain_row, weights):
    rows, width = normed.shape
    steps = weights.shape[1] // 2 // CHUNK
    whole = lambda k: (0, 0)
    return pl.pallas_call(
        segment_kernel,
        grid=(steps,),
        in_specs=[
            pl.BlockSpec((rows, width), whole),
            pl.BlockSpec((rows, width), whole),
            pl.BlockSpec((rows, width), whole),
            pl.BlockSpec((rows, 1), whole),
            pl.BlockSpec((1, width), whole),
            pl.BlockSpec((width, CHUNK), lambda k: (0, k)),
            pl.BlockSpec((width, CHUNK), lambda k: (0, k + steps)),
        ],
        out_specs=[pl.BlockSpec((rows, width), whole), pl.BlockSpec((1, width), whole)],
        out_shape=[
            jax.ShapeDtypeStruct((rows, width), jnp.bfloat16),
            jax.ShapeDtypeStruct((1, width), jnp.float32),
        ],
        scratch_shapes=[pltpu.VMEM((rows, width), jnp.float32)],
        cost_estimate=pl.CostEstimate(
            flops=6 * rows * width * weights.shape[1] // 2,
            transcendentals=rows * weights.shape[1] // 2,
            bytes_accessed=2 * weights.size + 12 * rows * width,
        ),
    )(normed, grad_in, standardized, inverse_deviation, gain_row, weights, weights)


def on_device(x_saved, gains, w_in, w_out, cotangent, lengths):
    rows = cotangent.shape[0]
    width = cotangent.shape[1]
    ends = jnp.cumsum(lengths)
    position = lax.axis_index(DP) * rows + jnp.arange(rows, dtype=jnp.int32)
    utter_hit = (position[:, None] >= ends[None, :]).astype(jnp.int32)
    utter = jnp.sum(utter_hit, 1)
    onehot = (utter[:, None] == jnp.arange(lengths.shape[0], dtype=jnp.int32)[None, :]).astype(
        jnp.int32
    )
    tok_len = jnp.sum(onehot * lengths[None, :], 1).astype(jnp.float32)
    weight = 2.0 * rows / (tok_len + rows)
    current = (cotangent.astype(jnp.float32) * weight[:, None]).astype(jnp.bfloat16)
    xf = x_saved[0].astype(jnp.float32)
    centered_input = xf - jnp.mean(xf, -1, keepdims=True)
    variance = jnp.mean(centered_input * centered_input, -1, keepdims=True)
    inverse_deviation = lax.rsqrt(variance + 1e-05)
    standardized_input = centered_input * inverse_deviation
    gain_vector = gains[0]
    normalized_input = (standardized_input * gain_vector).astype(jnp.bfloat16)
    local = jnp.concatenate([w_in[0], w_out[0].T], axis=1)
    weights = lax.all_gather(local, DP, axis=0, tiled=True)

    def block_back(grad_in):
        return segment_back(
            normalized_input, grad_in, standardized_input, inverse_deviation,
            gain_vector[None, :], weights,
        )

    def pass_through(grad_in):
        return (grad_in, jnp.zeros((1, width), jnp.float32))

    segments = lax.axis_size("segment")
    my_segment = lax.axis_index("segment")
    result = current
    gain_local = jnp.zeros((1, width), jnp.float32)
    for level in range(segments - 1, -1, -1):
        mine = my_segment == level
        updated, gain_partial = lax.cond(mine, block_back, pass_through, current)
        result = jnp.where(mine, updated, result)
        gain_local = jnp.where(mine, gain_partial, gain_local)
        if level > 0:
            current = lax.ppermute(updated, "segment", [(level, level - 1)])
    gain_total = lax.psum(lax.psum(lax.psum(gain_local, "core"), "y"), "z")
    return (result[None], gain_total)


def solution(mesh):
    n_seg, n_dp = mesh.devices.shape
    shape = (n_seg, n_dp // 8, 4, 2)
    mesh = Mesh(np.asarray(mesh.devices).reshape(shape), ("segment",) + DP)
    in_specs = (
        P("segment", DP, None),
        P("segment", None),
        P("segment", DP, None),
        P("segment", None, DP),
        P(DP, None),
        P(),
    )
    out_specs = (P("segment", DP, None), P("segment", None))
    return jax.shard_map(
        on_device, mesh=mesh, in_specs=in_specs, out_specs=out_specs, check_vma=False
    )
```

```python
import jax
import jax.numpy as jnp
import numpy as np
from jax import lax
from jax.experimental import pallas as pl
from jax.experimental.pallas import tpu as pltpu
from jax.sharding import Mesh, PartitionSpec as P

DP = ("z", "y", "core")
CHUNK = 768


def act_kernel(z_ref, w1_ref, act_ref):
    hidden = jnp.dot(z_ref[...], w1_ref[...], preferred_element_type=jnp.float32)
    sig = jax.nn.sigmoid(hidden)
    act_ref[...] = sig + hidden * sig * (1.0 - sig)


def hidden_slope(normed, weights):
    rows, width = normed.shape
    ff = weights.shape[1] // 2
    return pl.pallas_call(
        act_kernel,
        grid=(ff // CHUNK,),
        in_specs=[
            pl.BlockSpec((rows, width), lambda k: (0, 0)),
            pl.BlockSpec((width, CHUNK), lambda k: (0, k)),
        ],
        out_specs=pl.BlockSpec((rows, CHUNK), lambda k: (0, k)),
        out_shape=jax.ShapeDtypeStruct((rows, ff), jnp.float32),
        cost_estimate=pl.CostEstimate(
            flops=2 * rows * width * ff, transcendentals=rows * ff,
            bytes_accessed=2 * width * ff + 4 * rows * ff + 2 * rows * width,
        ),
    )(normed, weights)


def segment_kernel(g_ref, act_ref, xh_ref, inv_ref, gain_ref, w1_ref, w2_ref, out_ref, gp_ref, acc_ref):
    k = pl.program_id(0)

    @pl.when(k == 0)
    def _():
        acc_ref[...] = jnp.zeros_like(acc_ref)

    up_grad = jnp.dot(g_ref[...], w2_ref[...], preferred_element_type=jnp.float32)
    hid_grad = (0.5 * up_grad * act_ref[...]).astype(jnp.bfloat16)
    acc_ref[...] += lax.dot_general(
        hid_grad, w1_ref[...], (((1,), (1,)), ((), ())), preferred_element_type=jnp.float32
    )

    @pl.when(k == pl.num_programs(0) - 1)
    def _():
        norm_gradient = acc_ref[...]
        standardized = xh_ref[...]
        gp_ref[...] = jnp.sum(norm_gradient * standardized, axis=0, keepdims=True)
        gain_scaled = norm_gradient * gain_ref[...]
        mean_e = jnp.mean(gain_scaled, axis=-1, keepdims=True)
        mean_ex = jnp.mean(gain_scaled * standardized, axis=-1, keepdims=True)
        back = inv_ref[...] * (gain_scaled - mean_e - standardized * mean_ex)
        out_ref[...] = (g_ref[...].astype(jnp.float32) + back).astype(out_ref.dtype)


def segment_back(grad_in, slope, standardized, inverse_deviation, gain_row, weights):
    rows, width = grad_in.shape
    steps = weights.shape[1] // 2 // CHUNK
    whole = lambda k: (0, 0)
    return pl.pallas_call(
        segment_kernel,
        grid=(steps,),
        in_specs=[
            pl.BlockSpec((rows, width), whole),
            pl.BlockSpec((rows, CHUNK), lambda k: (0, k)),
            pl.BlockSpec((rows, width), whole),
            pl.BlockSpec((rows, 1), whole),
            pl.BlockSpec((1, width), whole),
            pl.BlockSpec((width, CHUNK), lambda k: (0, k)),
            pl.BlockSpec((width, CHUNK), lambda k: (0, k + steps)),
        ],
        out_specs=[pl.BlockSpec((rows, width), whole), pl.BlockSpec((1, width), whole)],
        out_shape=[
            jax.ShapeDtypeStruct((rows, width), jnp.bfloat16),
            jax.ShapeDtypeStruct((1, width), jnp.float32),
        ],
        scratch_shapes=[pltpu.VMEM((rows, width), jnp.float32)],
        cost_estimate=pl.CostEstimate(
            flops=4 * rows * width * weights.shape[1] // 2,
            transcendentals=0,
            bytes_accessed=2 * weights.size + 2 * rows * weights.shape[1] + 12 * rows * width,
        ),
    )(grad_in, slope, standardized, inverse_deviation, gain_row, weights, weights)


def on_device(x_saved, gains, w_in, w_out, cotangent, lengths):
    rows = cotangent.shape[0]
    width = cotangent.shape[1]
    ends = jnp.cumsum(lengths)
    position = lax.axis_index(DP) * rows + jnp.arange(rows, dtype=jnp.int32)
    utter_hit = (position[:, None] >= ends[None, :]).astype(jnp.int32)
    utter = jnp.sum(utter_hit, 1)
    onehot = (utter[:, None] == jnp.arange(lengths.shape[0], dtype=jnp.int32)[None, :]).astype(
        jnp.int32
    )
    tok_len = jnp.sum(onehot * lengths[None, :], 1).astype(jnp.float32)
    weight = 2.0 * rows / (tok_len + rows)
    current = (cotangent.astype(jnp.float32) * weight[:, None]).astype(jnp.bfloat16)
    xf = x_saved[0].astype(jnp.float32)
    centered_input = xf - jnp.mean(xf, -1, keepdims=True)
    variance = jnp.mean(centered_input * centered_input, -1, keepdims=True)
    inverse_deviation = lax.rsqrt(variance + 1e-05)
    standardized_input = centered_input * inverse_deviation
    gain_vector = gains[0]
    normalized_input = (standardized_input * gain_vector).astype(jnp.bfloat16)
    local = jnp.concatenate([w_in[0], w_out[0].T], axis=1)
    weights = lax.all_gather(local, DP, axis=0, tiled=True)

    slope = hidden_slope(normalized_input, weights)

    def block_back(grad_in):
        return segment_back(
            grad_in, slope, standardized_input, inverse_deviation, gain_vector[None, :], weights
        )

    def pass_through(grad_in):
        return (grad_in, jnp.zeros((1, width), jnp.float32))

    segments = lax.axis_size("segment")
    my_segment = lax.axis_index("segment")
    result = current
    gain_local = jnp.zeros((1, width), jnp.float32)
    for level in range(segments - 1, -1, -1):
        mine = my_segment == level
        updated, gain_partial = lax.cond(mine, block_back, pass_through, current)
        result = jnp.where(mine, updated, result)
        gain_local = jnp.where(mine, gain_partial, gain_local)
        if level > 0:
            current = lax.ppermute(updated, "segment", [(level, level - 1)])
    gain_total = lax.psum(lax.psum(lax.psum(gain_local, "core"), "y"), "z")
    return (result[None], gain_total)


def solution(mesh):
    n_seg, n_dp = mesh.devices.shape
    shape = (n_seg, n_dp // 8, 4, 2)
    mesh = Mesh(np.asarray(mesh.devices).reshape(shape), ("segment",) + DP)
    in_specs = (
        P("segment", DP, None),
        P("segment", None),
        P("segment", DP, None),
        P("segment", None, DP),
        P(DP, None),
        P(),
    )
    out_specs = (P("segment", DP, None), P("segment", None))
    return jax.shard_map(
        on_device, mesh=mesh, in_specs=in_specs, out_specs=out_specs, check_vma=False
    )
```

```python
import jax
import jax.numpy as jnp
import numpy as np
from jax import lax
from jax.experimental import pallas as pl
from jax.experimental.pallas import tpu as pltpu
from jax.sharding import Mesh, PartitionSpec as P

DP = ("z", "y", "core")
CHUNK = 768


def act_kernel(z_ref, w1_ref, act_ref):
    hidden = jnp.dot(z_ref[...], w1_ref[...], preferred_element_type=jnp.float32)
    sig = jax.nn.sigmoid(hidden)
    act_ref[...] = sig + hidden * sig * (1.0 - sig)


def hidden_slope(normed, weights):
    rows, width = normed.shape
    ff = weights.shape[1] // 2
    return pl.pallas_call(
        act_kernel,
        grid=(ff // CHUNK,),
        in_specs=[
            pl.BlockSpec((rows, width), lambda k: (0, 0)),
            pl.BlockSpec((width, CHUNK), lambda k: (0, k)),
        ],
        out_specs=pl.BlockSpec((rows, CHUNK), lambda k: (0, k)),
        out_shape=jax.ShapeDtypeStruct((rows, ff), jnp.float32),
        cost_estimate=pl.CostEstimate(
            flops=2 * rows * width * ff, transcendentals=rows * ff,
            bytes_accessed=2 * width * ff + 4 * rows * ff + 2 * rows * width,
        ),
    )(normed, weights)


def fused_kernel(z_ref, g_ref, xh_ref, inv_ref, gain_ref, w1_ref, w2_ref, out_ref, gp_ref, acc_ref):
    k = pl.program_id(0)

    @pl.when(k == 0)
    def _():
        acc_ref[...] = jnp.zeros_like(acc_ref)

    w1 = w1_ref[...]
    hidden = jnp.dot(z_ref[...], w1, preferred_element_type=jnp.float32)
    up_grad = jnp.dot(g_ref[...], w2_ref[...], preferred_element_type=jnp.float32)
    sig = jax.nn.sigmoid(hidden)
    hid_grad = (0.5 * up_grad * (sig + hidden * sig * (1.0 - sig))).astype(jnp.bfloat16)
    acc_ref[...] += lax.dot_general(
        hid_grad, w1, (((1,), (1,)), ((), ())), preferred_element_type=jnp.float32
    )

    @pl.when(k == pl.num_programs(0) - 1)
    def _():
        norm_backward(acc_ref, xh_ref, inv_ref, gain_ref, g_ref, out_ref, gp_ref)


def norm_backward(acc_ref, xh_ref, inv_ref, gain_ref, g_ref, out_ref, gp_ref):
    norm_gradient = acc_ref[...]
    standardized = xh_ref[...]
    gp_ref[...] = jnp.sum(norm_gradient * standardized, axis=0, keepdims=True)
    gain_scaled = norm_gradient * gain_ref[...]
    mean_e = jnp.mean(gain_scaled, axis=-1, keepdims=True)
    mean_ex = jnp.mean(gain_scaled * standardized, axis=-1, keepdims=True)
    back = inv_ref[:, 0:1] * (gain_scaled - mean_e - standardized * mean_ex)
    out_ref[...] = (g_ref[...].astype(jnp.float32) + back).astype(out_ref.dtype)


def fused_back(normed, grad_in, standardized, inverse_deviation, gain_row, weights):
    rows, width = normed.shape
    steps = weights.shape[1] // 2 // CHUNK
    whole = lambda k: (0, 0)
    return pl.pallas_call(
        fused_kernel,
        grid=(steps,),
        in_specs=[
            pl.BlockSpec((rows, width), whole),
            pl.BlockSpec((rows, width), whole),
            pl.BlockSpec((rows, width), whole),
            pl.BlockSpec(inverse_deviation.shape, whole),
            pl.BlockSpec((1, width), whole),
            pl.BlockSpec((width, CHUNK), lambda k: (0, k)),
            pl.BlockSpec((width, CHUNK), lambda k: (0, k + steps)),
        ],
        out_specs=[pl.BlockSpec((rows, width), whole), pl.BlockSpec((1, width), whole)],
        out_shape=[
            jax.ShapeDtypeStruct((rows, width), jnp.bfloat16),
            jax.ShapeDtypeStruct((1, width), jnp.float32),
        ],
        scratch_shapes=[pltpu.VMEM((rows, width), jnp.float32)],
        cost_estimate=pl.CostEstimate(
            flops=6 * rows * width * weights.shape[1] // 2,
            transcendentals=rows * weights.shape[1] // 2,
            bytes_accessed=2 * weights.size + 12 * rows * width,
        ),
    )(normed, grad_in, standardized, inverse_deviation, gain_row, weights, weights)


def segment_kernel(g_ref, act_ref, xh_ref, inv_ref, gain_ref, w1_ref, w2_ref, out_ref, gp_ref, acc_ref):
    k = pl.program_id(0)

    @pl.when(k == 0)
    def _():
        acc_ref[...] = jnp.zeros_like(acc_ref)

    up_grad = jnp.dot(g_ref[...], w2_ref[...], preferred_element_type=jnp.float32)
    hid_grad = (0.5 * up_grad * act_ref[...]).astype(jnp.bfloat16)
    acc_ref[...] += lax.dot_general(
        hid_grad, w1_ref[...], (((1,), (1,)), ((), ())), preferred_element_type=jnp.float32
    )

    @pl.when(k == pl.num_programs(0) - 1)
    def _():
        norm_backward(acc_ref, xh_ref, inv_ref, gain_ref, g_ref, out_ref, gp_ref)


def segment_back(grad_in, slope, standardized, inverse_deviation, gain_row, weights):
    rows, width = grad_in.shape
    steps = weights.shape[1] // 2 // CHUNK
    whole = lambda k: (0, 0)
    return pl.pallas_call(
        segment_kernel,
        grid=(steps,),
        in_specs=[
            pl.BlockSpec((rows, width), whole),
            pl.BlockSpec((rows, CHUNK), lambda k: (0, k)),
            pl.BlockSpec((rows, width), whole),
            pl.BlockSpec(inverse_deviation.shape, whole),
            pl.BlockSpec((1, width), whole),
            pl.BlockSpec((width, CHUNK), lambda k: (0, k)),
            pl.BlockSpec((width, CHUNK), lambda k: (0, k + steps)),
        ],
        out_specs=[pl.BlockSpec((rows, width), whole), pl.BlockSpec((1, width), whole)],
        out_shape=[
            jax.ShapeDtypeStruct((rows, width), jnp.bfloat16),
            jax.ShapeDtypeStruct((1, width), jnp.float32),
        ],
        scratch_shapes=[pltpu.VMEM((rows, width), jnp.float32)],
        cost_estimate=pl.CostEstimate(
            flops=4 * rows * width * weights.shape[1] // 2,
            transcendentals=0,
            bytes_accessed=2 * weights.size + 2 * rows * weights.shape[1] + 12 * rows * width,
        ),
    )(grad_in, slope, standardized, inverse_deviation, gain_row, weights, weights)


def on_device(x_saved, gains, w_in, w_out, cotangent, lengths):
    rows = cotangent.shape[0]
    width = cotangent.shape[1]
    ends = jnp.cumsum(lengths)
    position = lax.axis_index(DP) * rows + jnp.arange(rows, dtype=jnp.int32)
    utter_hit = (position[:, None] >= ends[None, :]).astype(jnp.int32)
    utter = jnp.sum(utter_hit, 1)
    onehot = (utter[:, None] == jnp.arange(lengths.shape[0], dtype=jnp.int32)[None, :]).astype(
        jnp.int32
    )
    tok_len = jnp.sum(onehot * lengths[None, :], 1).astype(jnp.float32)
    weight = 2.0 * rows / (tok_len + rows)
    current = (cotangent.astype(jnp.float32) * weight[:, None]).astype(jnp.bfloat16)
    xf = x_saved[0].astype(jnp.float32)
    centered_input = xf - jnp.mean(xf, -1, keepdims=True)
    variance = jnp.mean(centered_input * centered_input, -1, keepdims=True)
    inverse_deviation = lax.rsqrt(variance + 1e-05)
    standardized_input = centered_input * inverse_deviation
    gain_vector = gains[0]
    normalized_input = (standardized_input * gain_vector).astype(jnp.bfloat16)
    local = jnp.concatenate([w_in[0], w_out[0].T], axis=1)
    weights = lax.all_gather(local, DP, axis=0, tiled=True)

    inverse_rows = jnp.broadcast_to(inverse_deviation, (rows, 128))
    gain_row = gain_vector[None, :]
    segments = lax.axis_size("segment")
    my_segment = lax.axis_index("segment")
    first = segments - 1
    slope = lax.cond(
        my_segment == first,
        lambda: jnp.zeros((rows, weights.shape[1] // 2), jnp.float32),
        lambda: hidden_slope(normalized_input, weights),
    )

    def keep(grad_in, kept, kept_gain):
        return kept, kept_gain

    result = current
    gain_local = jnp.zeros((1, width), jnp.float32)
    for level in range(first, -1, -1):
        if level == first:
            def mine(grad_in, kept, kept_gain):
                return fused_back(
                    normalized_input, grad_in, standardized_input, inverse_rows, gain_row, weights
                )
        else:
            def mine(grad_in, kept, kept_gain):
                return segment_back(
                    grad_in, slope, standardized_input, inverse_rows, gain_row, weights
                )
        result, gain_local = lax.cond(
            my_segment == level, mine, keep, current, result, gain_local
        )
        if level > 0:
            current = lax.ppermute(result, "segment", [(level, level - 1)])
    gain_total = lax.psum(lax.psum(lax.psum(gain_local, "core"), "y"), "z")
    return (result[None], gain_total)


def solution(mesh):
    n_seg, n_dp = mesh.devices.shape
    shape = (n_seg, n_dp // 8, 4, 2)
    mesh = Mesh(np.asarray(mesh.devices).reshape(shape), ("segment",) + DP)
    in_specs = (
        P("segment", DP, None),
        P("segment", None),
        P("segment", DP, None),
        P("segment", None, DP),
        P(DP, None),
        P(),
    )
    out_specs = (P("segment", DP, None), P("segment", None))
    return jax.shard_map(
        on_device, mesh=mesh, in_specs=in_specs, out_specs=out_specs, check_vma=False
    )
```

```python
import jax
import jax.numpy as jnp
import numpy as np
from jax import lax
from jax.experimental import pallas as pl
from jax.experimental.pallas import tpu as pltpu
from jax.sharding import Mesh, PartitionSpec as P

DP = ("z", "y", "core")
CHUNK = 768


def act_kernel(z_ref, w1_ref, act_ref):
    hidden = jnp.dot(z_ref[...], w1_ref[...], preferred_element_type=jnp.float32)
    sig = jax.nn.sigmoid(hidden)
    act_ref[...] = (sig + hidden * sig * (1.0 - sig)).astype(act_ref.dtype)


def hidden_slope(normed, weights):
    rows, width = normed.shape
    ff = weights.shape[1] // 2
    return pl.pallas_call(
        act_kernel,
        grid=(ff // CHUNK,),
        in_specs=[
            pl.BlockSpec((rows, width), lambda k: (0, 0)),
            pl.BlockSpec((width, CHUNK), lambda k: (0, k)),
        ],
        out_specs=pl.BlockSpec((rows, CHUNK), lambda k: (0, k)),
        out_shape=jax.ShapeDtypeStruct((rows, ff), jnp.bfloat16),
        cost_estimate=pl.CostEstimate(
            flops=2 * rows * width * ff, transcendentals=rows * ff,
            bytes_accessed=2 * width * ff + 2 * rows * ff + 2 * rows * width,
        ),
    )(normed, weights)


def fused_kernel(z_ref, g_ref, xh_ref, inv_ref, gain_ref, w1_ref, w2_ref, out_ref, gp_ref, acc_ref):
    k = pl.program_id(0)

    @pl.when(k == 0)
    def _():
        acc_ref[...] = jnp.zeros_like(acc_ref)

    w1 = w1_ref[...]
    hidden = jnp.dot(z_ref[...], w1, preferred_element_type=jnp.float32)
    up_grad = jnp.dot(g_ref[...], w2_ref[...], preferred_element_type=jnp.float32)
    sig = jax.nn.sigmoid(hidden)
    hid_grad = (0.5 * up_grad * (sig + hidden * sig * (1.0 - sig))).astype(jnp.bfloat16)
    acc_ref[...] += lax.dot_general(
        hid_grad, w1, (((1,), (1,)), ((), ())), preferred_element_type=jnp.float32
    )

    @pl.when(k == pl.num_programs(0) - 1)
    def _():
        norm_backward(acc_ref, xh_ref, inv_ref, gain_ref, g_ref, out_ref, gp_ref)


def norm_backward(acc_ref, xh_ref, inv_ref, gain_ref, g_ref, out_ref, gp_ref):
    norm_gradient = acc_ref[...]
    standardized = xh_ref[...]
    gp_ref[...] = jnp.sum(norm_gradient * standardized, axis=0, keepdims=True)
    gain_scaled = norm_gradient * gain_ref[...]
    mean_e = jnp.mean(gain_scaled, axis=-1, keepdims=True)
    mean_ex = jnp.mean(gain_scaled * standardized, axis=-1, keepdims=True)
    back = inv_ref[:, 0:1] * (gain_scaled - mean_e - standardized * mean_ex)
    out_ref[...] = (g_ref[...].astype(jnp.float32) + back).astype(out_ref.dtype)


def fused_back(normed, grad_in, standardized, inverse_deviation, gain_row, weights):
    rows, width = normed.shape
    steps = weights.shape[1] // 2 // CHUNK
    whole = lambda k: (0, 0)
    return pl.pallas_call(
        fused_kernel,
        grid=(steps,),
        in_specs=[
            pl.BlockSpec((rows, width), whole),
            pl.BlockSpec((rows, width), whole),
            pl.BlockSpec((rows, width), whole),
            pl.BlockSpec(inverse_deviation.shape, whole),
            pl.BlockSpec((1, width), whole),
            pl.BlockSpec((width, CHUNK), lambda k: (0, k)),
            pl.BlockSpec((width, CHUNK), lambda k: (0, k + steps)),
        ],
        out_specs=[pl.BlockSpec((rows, width), whole), pl.BlockSpec((1, width), whole)],
        out_shape=[
            jax.ShapeDtypeStruct((rows, width), jnp.bfloat16),
            jax.ShapeDtypeStruct((1, width), jnp.float32),
        ],
        scratch_shapes=[pltpu.VMEM((rows, width), jnp.float32)],
        cost_estimate=pl.CostEstimate(
            flops=6 * rows * width * weights.shape[1] // 2,
            transcendentals=rows * weights.shape[1] // 2,
            bytes_accessed=2 * weights.size + 12 * rows * width,
        ),
    )(normed, grad_in, standardized, inverse_deviation, gain_row, weights, weights)


def segment_kernel(g_ref, act_ref, xh_ref, inv_ref, gain_ref, w1_ref, w2_ref, out_ref, gp_ref, acc_ref):
    k = pl.program_id(0)

    @pl.when(k == 0)
    def _():
        acc_ref[...] = jnp.zeros_like(acc_ref)

    up_grad = jnp.dot(g_ref[...], w2_ref[...], preferred_element_type=jnp.float32)
    hid_grad = (0.5 * up_grad * act_ref[...].astype(jnp.float32)).astype(jnp.bfloat16)
    acc_ref[...] += lax.dot_general(
        hid_grad, w1_ref[...], (((1,), (1,)), ((), ())), preferred_element_type=jnp.float32
    )

    @pl.when(k == pl.num_programs(0) - 1)
    def _():
        norm_backward(acc_ref, xh_ref, inv_ref, gain_ref, g_ref, out_ref, gp_ref)


def segment_back(grad_in, slope, standardized, inverse_deviation, gain_row, weights):
    rows, width = grad_in.shape
    steps = weights.shape[1] // 2 // CHUNK
    whole = lambda k: (0, 0)
    return pl.pallas_call(
        segment_kernel,
        grid=(steps,),
        in_specs=[
            pl.BlockSpec((rows, width), whole),
            pl.BlockSpec((rows, CHUNK), lambda k: (0, k)),
            pl.BlockSpec((rows, width), whole),
            pl.BlockSpec(inverse_deviation.shape, whole),
            pl.BlockSpec((1, width), whole),
            pl.BlockSpec((width, CHUNK), lambda k: (0, k)),
            pl.BlockSpec((width, CHUNK), lambda k: (0, k + steps)),
        ],
        out_specs=[pl.BlockSpec((rows, width), whole), pl.BlockSpec((1, width), whole)],
        out_shape=[
            jax.ShapeDtypeStruct((rows, width), jnp.bfloat16),
            jax.ShapeDtypeStruct((1, width), jnp.float32),
        ],
        scratch_shapes=[pltpu.VMEM((rows, width), jnp.float32)],
        cost_estimate=pl.CostEstimate(
            flops=4 * rows * width * weights.shape[1] // 2,
            transcendentals=0,
            bytes_accessed=2 * weights.size + 2 * rows * weights.shape[1] + 12 * rows * width,
        ),
    )(grad_in, slope, standardized, inverse_deviation, gain_row, weights, weights)


def on_device(x_saved, gains, w_in, w_out, cotangent, lengths):
    rows = cotangent.shape[0]
    width = cotangent.shape[1]
    ends = jnp.cumsum(lengths)
    position = lax.axis_index(DP) * rows + jnp.arange(rows, dtype=jnp.int32)
    utter_hit = (position[:, None] >= ends[None, :]).astype(jnp.int32)
    utter = jnp.sum(utter_hit, 1)
    onehot = (utter[:, None] == jnp.arange(lengths.shape[0], dtype=jnp.int32)[None, :]).astype(
        jnp.int32
    )
    tok_len = jnp.sum(onehot * lengths[None, :], 1).astype(jnp.float32)
    weight = 2.0 * rows / (tok_len + rows)
    current = (cotangent.astype(jnp.float32) * weight[:, None]).astype(jnp.bfloat16)
    xf = x_saved[0].astype(jnp.float32)
    centered_input = xf - jnp.mean(xf, -1, keepdims=True)
    variance = jnp.mean(centered_input * centered_input, -1, keepdims=True)
    inverse_deviation = lax.rsqrt(variance + 1e-05)
    standardized_input = centered_input * inverse_deviation
    gain_vector = gains[0]
    normalized_input = (standardized_input * gain_vector).astype(jnp.bfloat16)
    eye = jnp.eye(w_out.shape[2], dtype=w_out.dtype)
    w_out_t = lax.dot_general(
        eye, w_out[0], (((1,), (1,)), ((), ())), preferred_element_type=jnp.float32
    ).astype(w_out.dtype)
    local = jnp.concatenate([w_in[0], w_out_t], axis=1)
    weights = lax.all_gather(local, DP, axis=0, tiled=True)

    inverse_rows = jnp.broadcast_to(inverse_deviation, (rows, 128))
    gain_row = gain_vector[None, :]
    segments = lax.axis_size("segment")
    my_segment = lax.axis_index("segment")
    first = segments - 1
    slope = lax.cond(
        my_segment == first,
        lambda: jnp.zeros((rows, weights.shape[1] // 2), jnp.bfloat16),
        lambda: hidden_slope(normalized_input, weights),
    )

    def keep(grad_in, kept, kept_gain):
        return kept, kept_gain

    result = current
    gain_local = jnp.zeros((1, width), jnp.float32)
    for level in range(first, -1, -1):
        if level == first:
            def mine(grad_in, kept, kept_gain):
                return fused_back(
                    normalized_input, grad_in, standardized_input, inverse_rows, gain_row, weights
                )
        else:
            def mine(grad_in, kept, kept_gain):
                return segment_back(
                    grad_in, slope, standardized_input, inverse_rows, gain_row, weights
                )
        result, gain_local = lax.cond(
            my_segment == level, mine, keep, current, result, gain_local
        )
        if level > 0:
            current = lax.ppermute(result, "segment", [(level, level - 1)])
    gain_total = lax.psum(lax.psum(lax.psum(gain_local, "core"), "y"), "z")
    return (result[None], gain_total)


def solution(mesh):
    n_seg, n_dp = mesh.devices.shape
    shape = (n_seg, n_dp // 8, 4, 2)
    mesh = Mesh(np.asarray(mesh.devices).reshape(shape), ("segment",) + DP)
    in_specs = (
        P("segment", DP, None),
        P("segment", None),
        P("segment", DP, None),
        P("segment", None, DP),
        P(DP, None),
        P(),
    )
    out_specs = (P("segment", DP, None), P("segment", None))
    return jax.shard_map(
        on_device, mesh=mesh, in_specs=in_specs, out_specs=out_specs, check_vma=False
    )
```

```python
import jax
import jax.numpy as jnp
import numpy as np
from jax import lax
from jax.experimental import pallas as pl
from jax.experimental.pallas import tpu as pltpu
from jax.sharding import Mesh, PartitionSpec as P

DP = ("z", "y", "core")
CHUNK = 768


def act_kernel(z_ref, w1_ref, act_ref):
    hidden = jnp.dot(z_ref[...], w1_ref[...], preferred_element_type=jnp.float32)
    sig = jax.nn.sigmoid(hidden)
    act_ref[...] = (sig + hidden * sig * (1.0 - sig)).astype(act_ref.dtype)


def hidden_slope(normed, weights):
    rows, width = normed.shape
    ff = weights.shape[1] // 2
    return pl.pallas_call(
        act_kernel,
        grid=(ff // CHUNK,),
        in_specs=[
            pl.BlockSpec((rows, width), lambda k: (0, 0)),
            pl.BlockSpec((width, CHUNK), lambda k: (0, k)),
        ],
        out_specs=pl.BlockSpec((rows, CHUNK), lambda k: (0, k)),
        out_shape=jax.ShapeDtypeStruct((rows, ff), jnp.bfloat16),
        cost_estimate=pl.CostEstimate(
            flops=2 * rows * width * ff, transcendentals=rows * ff,
            bytes_accessed=2 * width * ff + 2 * rows * ff + 2 * rows * width,
        ),
    )(normed, weights)


def fused_kernel(z_ref, g_ref, xh_ref, inv_ref, gain_ref, w1_ref, w2_ref, out_ref, gp_ref, acc_ref):
    k = pl.program_id(0)

    @pl.when(k == 0)
    def _():
        acc_ref[...] = jnp.zeros_like(acc_ref)

    w1 = w1_ref[...]
    hidden = jnp.dot(z_ref[...], w1, preferred_element_type=jnp.float32)
    up_grad = jnp.dot(g_ref[...], w2_ref[...], preferred_element_type=jnp.float32)
    sig = jax.nn.sigmoid(hidden)
    hid_grad = (0.5 * up_grad * (sig + hidden * sig * (1.0 - sig))).astype(jnp.bfloat16)
    acc_ref[...] += lax.dot_general(
        hid_grad, w1, (((1,), (1,)), ((), ())), preferred_element_type=jnp.float32
    )

    @pl.when(k == pl.num_programs(0) - 1)
    def _():
        norm_backward(acc_ref, xh_ref, inv_ref, gain_ref, g_ref, out_ref, gp_ref)


def norm_backward(acc_ref, xh_ref, inv_ref, gain_ref, g_ref, out_ref, gp_ref):
    norm_gradient = acc_ref[...]
    standardized = xh_ref[...]
    gp_ref[...] = jnp.sum(norm_gradient * standardized, axis=0, keepdims=True)
    gain_scaled = norm_gradient * gain_ref[...]
    mean_e = jnp.mean(gain_scaled, axis=-1, keepdims=True)
    mean_ex = jnp.mean(gain_scaled * standardized, axis=-1, keepdims=True)
    back = inv_ref[:, 0:1] * (gain_scaled - mean_e - standardized * mean_ex)
    out_ref[...] = (g_ref[...].astype(jnp.float32) + back).astype(out_ref.dtype)


def fused_back(normed, grad_in, standardized, inverse_deviation, gain_row, weights):
    rows, width = normed.shape
    steps = weights.shape[1] // 2 // CHUNK
    whole = lambda k: (0, 0)
    return pl.pallas_call(
        fused_kernel,
        grid=(steps,),
        in_specs=[
            pl.BlockSpec((rows, width), whole),
            pl.BlockSpec((rows, width), whole),
            pl.BlockSpec((rows, width), whole),
            pl.BlockSpec(inverse_deviation.shape, whole),
            pl.BlockSpec((1, width), whole),
            pl.BlockSpec((width, CHUNK), lambda k: (0, k)),
            pl.BlockSpec((width, CHUNK), lambda k: (0, k + steps)),
        ],
        out_specs=[pl.BlockSpec((rows, width), whole), pl.BlockSpec((1, width), whole)],
        out_shape=[
            jax.ShapeDtypeStruct((rows, width), jnp.bfloat16),
            jax.ShapeDtypeStruct((1, width), jnp.float32),
        ],
        scratch_shapes=[pltpu.VMEM((rows, width), jnp.float32)],
        cost_estimate=pl.CostEstimate(
            flops=6 * rows * width * weights.shape[1] // 2,
            transcendentals=rows * weights.shape[1] // 2,
            bytes_accessed=2 * weights.size + 12 * rows * width,
        ),
    )(normed, grad_in, standardized, inverse_deviation, gain_row, weights, weights)


def segment_kernel(g_ref, act_ref, xh_ref, inv_ref, gain_ref, w1_ref, w2_ref, out_ref, gp_ref, acc_ref):
    k = pl.program_id(0)

    @pl.when(k == 0)
    def _():
        acc_ref[...] = jnp.zeros_like(acc_ref)

    up_grad = jnp.dot(g_ref[...], w2_ref[...], preferred_element_type=jnp.float32)
    hid_grad = (0.5 * up_grad * act_ref[...].astype(jnp.float32)).astype(jnp.bfloat16)
    acc_ref[...] += lax.dot_general(
        hid_grad, w1_ref[...], (((1,), (1,)), ((), ())), preferred_element_type=jnp.float32
    )

    @pl.when(k == pl.num_programs(0) - 1)
    def _():
        norm_backward(acc_ref, xh_ref, inv_ref, gain_ref, g_ref, out_ref, gp_ref)


def segment_back(grad_in, slope, standardized, inverse_deviation, gain_row, weights):
    rows, width = grad_in.shape
    steps = weights.shape[1] // 2 // CHUNK
    whole = lambda k: (0, 0)
    return pl.pallas_call(
        segment_kernel,
        grid=(steps,),
        in_specs=[
            pl.BlockSpec((rows, width), whole),
            pl.BlockSpec((rows, CHUNK), lambda k: (0, k)),
            pl.BlockSpec((rows, width), whole),
            pl.BlockSpec(inverse_deviation.shape, whole),
            pl.BlockSpec((1, width), whole),
            pl.BlockSpec((width, CHUNK), lambda k: (0, k)),
            pl.BlockSpec((width, CHUNK), lambda k: (0, k + steps)),
        ],
        out_specs=[pl.BlockSpec((rows, width), whole), pl.BlockSpec((1, width), whole)],
        out_shape=[
            jax.ShapeDtypeStruct((rows, width), jnp.bfloat16),
            jax.ShapeDtypeStruct((1, width), jnp.float32),
        ],
        scratch_shapes=[pltpu.VMEM((rows, width), jnp.float32)],
        cost_estimate=pl.CostEstimate(
            flops=4 * rows * width * weights.shape[1] // 2,
            transcendentals=0,
            bytes_accessed=2 * weights.size + 2 * rows * weights.shape[1] + 12 * rows * width,
        ),
    )(grad_in, slope, standardized, inverse_deviation, gain_row, weights, weights)


def on_device(x_saved, gains, w_in, w_out, cotangent, lengths):
    rows = cotangent.shape[0]
    width = cotangent.shape[1]
    ends = jnp.cumsum(lengths)
    position = lax.axis_index(DP) * rows + jnp.arange(rows, dtype=jnp.int32)
    utter_hit = (position[:, None] >= ends[None, :]).astype(jnp.int32)
    utter = jnp.sum(utter_hit, 1)
    onehot = (utter[:, None] == jnp.arange(lengths.shape[0], dtype=jnp.int32)[None, :]).astype(
        jnp.int32
    )
    tok_len = jnp.sum(onehot * lengths[None, :], 1).astype(jnp.float32)
    weight = 2.0 * rows / (tok_len + rows)
    current = (cotangent.astype(jnp.float32) * weight[:, None]).astype(jnp.bfloat16)
    xf = x_saved[0].astype(jnp.float32)
    centered_input = xf - jnp.mean(xf, -1, keepdims=True)
    variance = jnp.mean(centered_input * centered_input, -1, keepdims=True)
    inverse_deviation = lax.rsqrt(variance + 1e-05)
    standardized_input = centered_input * inverse_deviation
    gain_vector = gains[0]
    normalized_input = (standardized_input * gain_vector).astype(jnp.bfloat16)
    local = jnp.concatenate([w_in[0], w_out[0].T], axis=1)
    weights = lax.all_gather(local, DP, axis=0, tiled=True)

    inverse_rows = jnp.broadcast_to(inverse_deviation, (rows, 128))
    gain_row = gain_vector[None, :]
    segments = lax.axis_size("segment")
    my_segment = lax.axis_index("segment")
    first = segments - 1
    slope = lax.cond(
        my_segment == first,
        lambda: jnp.zeros((rows, weights.shape[1] // 2), jnp.bfloat16),
        lambda: hidden_slope(normalized_input, weights),
    )

    def keep(grad_in, kept, kept_gain):
        return kept, kept_gain

    result = current
    gain_local = jnp.zeros((1, width), jnp.float32)
    for level in range(first, -1, -1):
        if level == first:
            def mine(grad_in, kept, kept_gain):
                return fused_back(
                    normalized_input, grad_in, standardized_input, inverse_rows, gain_row, weights
                )
        else:
            def mine(grad_in, kept, kept_gain):
                return segment_back(
                    grad_in, slope, standardized_input, inverse_rows, gain_row, weights
                )
        result, gain_local = lax.cond(
            my_segment == level, mine, keep, current, result, gain_local
        )
        if level > 0:
            current = lax.ppermute(result, "segment", [(level, level - 1)])
    gain_total = lax.psum(lax.psum(lax.psum(gain_local, "core"), "y"), "z")
    return (result[None], gain_total)


def solution(mesh):
    n_seg, n_dp = mesh.devices.shape
    shape = (n_seg, n_dp // 8, 4, 2)
    mesh = Mesh(np.asarray(mesh.devices).reshape(shape), ("segment",) + DP)
    in_specs = (
        P("segment", DP, None),
        P("segment", None),
        P("segment", DP, None),
        P("segment", None, DP),
        P(DP, None),
        P(),
    )
    out_specs = (P("segment", DP, None), P("segment", None))
    return jax.shard_map(
        on_device, mesh=mesh, in_specs=in_specs, out_specs=out_specs, check_vma=False
    )
```

```python
import jax
import jax.numpy as jnp
import numpy as np
from jax import lax
from jax.experimental import pallas as pl
from jax.experimental.pallas import tpu as pltpu
from jax.sharding import Mesh, PartitionSpec as P

DP = ("z", "y", "core")
CHUNK = 768


def act_kernel(z_ref, w1_ref, act_ref):
    hidden = jnp.dot(z_ref[...], w1_ref[...], preferred_element_type=jnp.float32)
    sig = jax.nn.sigmoid(hidden)
    act_ref[...] = (sig + hidden * sig * (1.0 - sig)).astype(act_ref.dtype)


def hidden_slope(normed, weights):
    rows, width = normed.shape
    ff = weights.shape[1] // 2
    return pl.pallas_call(
        act_kernel,
        grid=(ff // CHUNK,),
        in_specs=[
            pl.BlockSpec((rows, width), lambda k: (0, 0)),
            pl.BlockSpec((width, CHUNK), lambda k: (0, k)),
        ],
        out_specs=pl.BlockSpec((rows, CHUNK), lambda k: (0, k)),
        out_shape=jax.ShapeDtypeStruct((rows, ff), jnp.bfloat16),
        cost_estimate=pl.CostEstimate(
            flops=2 * rows * width * ff, transcendentals=rows * ff,
            bytes_accessed=2 * width * ff + 2 * rows * ff + 2 * rows * width,
        ),
    )(normed, weights)


def fused_kernel(
    x_ref, g_ref, mean_ref, inv_ref, gain_ref, w1_ref, w2_ref, out_ref, gp_ref, acc_ref, z_ref
):
    k = pl.program_id(0)

    @pl.when(k == 0)
    def _():
        acc_ref[...] = jnp.zeros_like(acc_ref)
        z_ref[...] = (standardize(x_ref, mean_ref, inv_ref) * gain_ref[...]).astype(z_ref.dtype)

    w1 = w1_ref[...]
    hidden = jnp.dot(z_ref[...], w1, preferred_element_type=jnp.float32)
    up_grad = jnp.dot(g_ref[...], w2_ref[...], preferred_element_type=jnp.float32)
    sig = jax.nn.sigmoid(hidden)
    hid_grad = (0.5 * up_grad * (sig + hidden * sig * (1.0 - sig))).astype(jnp.bfloat16)
    acc_ref[...] += lax.dot_general(
        hid_grad, w1, (((1,), (1,)), ((), ())), preferred_element_type=jnp.float32
    )

    @pl.when(k == pl.num_programs(0) - 1)
    def _():
        norm_backward(acc_ref, x_ref, mean_ref, inv_ref, gain_ref, g_ref, out_ref, gp_ref)


def standardize(x_ref, mean_ref, inv_ref):
    return (x_ref[...].astype(jnp.float32) - mean_ref[:, 0:1]) * inv_ref[:, 0:1]


def norm_backward(acc_ref, x_ref, mean_ref, inv_ref, gain_ref, g_ref, out_ref, gp_ref):
    norm_gradient = acc_ref[...]
    standardized = standardize(x_ref, mean_ref, inv_ref)
    gp_ref[...] = jnp.sum(norm_gradient * standardized, axis=0, keepdims=True)
    gain_scaled = norm_gradient * gain_ref[...]
    mean_e = jnp.mean(gain_scaled, axis=-1, keepdims=True)
    mean_ex = jnp.mean(gain_scaled * standardized, axis=-1, keepdims=True)
    back = inv_ref[:, 0:1] * (gain_scaled - mean_e - standardized * mean_ex)
    out_ref[...] = (g_ref[...].astype(jnp.float32) + back).astype(out_ref.dtype)


def fused_back(saved, grad_in, mean_rows, inverse_deviation, gain_row, weights):
    rows, width = saved.shape
    steps = weights.shape[1] // 2 // CHUNK
    whole = lambda k: (0, 0)
    return pl.pallas_call(
        fused_kernel,
        grid=(steps,),
        in_specs=[
            pl.BlockSpec((rows, width), whole),
            pl.BlockSpec((rows, width), whole),
            pl.BlockSpec(mean_rows.shape, whole),
            pl.BlockSpec(inverse_deviation.shape, whole),
            pl.BlockSpec((1, width), whole),
            pl.BlockSpec((width, CHUNK), lambda k: (0, k)),
            pl.BlockSpec((width, CHUNK), lambda k: (0, k + steps)),
        ],
        out_specs=[pl.BlockSpec((rows, width), whole), pl.BlockSpec((1, width), whole)],
        out_shape=[
            jax.ShapeDtypeStruct((rows, width), jnp.bfloat16),
            jax.ShapeDtypeStruct((1, width), jnp.float32),
        ],
        scratch_shapes=[
            pltpu.VMEM((rows, width), jnp.float32),
            pltpu.VMEM((rows, width), jnp.bfloat16),
        ],
        cost_estimate=pl.CostEstimate(
            flops=6 * rows * width * weights.shape[1] // 2,
            transcendentals=rows * weights.shape[1] // 2,
            bytes_accessed=2 * weights.size + 12 * rows * width,
        ),
    )(saved, grad_in, mean_rows, inverse_deviation, gain_row, weights, weights)


def segment_kernel(
    g_ref, act_ref, x_ref, mean_ref, inv_ref, gain_ref, w1_ref, w2_ref, out_ref, gp_ref, acc_ref
):
    k = pl.program_id(0)

    @pl.when(k == 0)
    def _():
        acc_ref[...] = jnp.zeros_like(acc_ref)

    up_grad = jnp.dot(g_ref[...], w2_ref[...], preferred_element_type=jnp.float32)
    hid_grad = (0.5 * up_grad * act_ref[...].astype(jnp.float32)).astype(jnp.bfloat16)
    acc_ref[...] += lax.dot_general(
        hid_grad, w1_ref[...], (((1,), (1,)), ((), ())), preferred_element_type=jnp.float32
    )

    @pl.when(k == pl.num_programs(0) - 1)
    def _():
        norm_backward(acc_ref, x_ref, mean_ref, inv_ref, gain_ref, g_ref, out_ref, gp_ref)


def segment_back(grad_in, slope, saved, mean_rows, inverse_deviation, gain_row, weights):
    rows, width = grad_in.shape
    steps = weights.shape[1] // 2 // CHUNK
    whole = lambda k: (0, 0)
    return pl.pallas_call(
        segment_kernel,
        grid=(steps,),
        in_specs=[
            pl.BlockSpec((rows, width), whole),
            pl.BlockSpec((rows, CHUNK), lambda k: (0, k)),
            pl.BlockSpec((rows, width), whole),
            pl.BlockSpec(mean_rows.shape, whole),
            pl.BlockSpec(inverse_deviation.shape, whole),
            pl.BlockSpec((1, width), whole),
            pl.BlockSpec((width, CHUNK), lambda k: (0, k)),
            pl.BlockSpec((width, CHUNK), lambda k: (0, k + steps)),
        ],
        out_specs=[pl.BlockSpec((rows, width), whole), pl.BlockSpec((1, width), whole)],
        out_shape=[
            jax.ShapeDtypeStruct((rows, width), jnp.bfloat16),
            jax.ShapeDtypeStruct((1, width), jnp.float32),
        ],
        scratch_shapes=[pltpu.VMEM((rows, width), jnp.float32)],
        cost_estimate=pl.CostEstimate(
            flops=4 * rows * width * weights.shape[1] // 2,
            transcendentals=0,
            bytes_accessed=2 * weights.size + 2 * rows * weights.shape[1] + 12 * rows * width,
        ),
    )(grad_in, slope, saved, mean_rows, inverse_deviation, gain_row, weights, weights)


def on_device(x_saved, gains, w_in, w_out, cotangent, lengths):
    rows = cotangent.shape[0]
    width = cotangent.shape[1]
    ends = jnp.cumsum(lengths)
    position = lax.axis_index(DP) * rows + jnp.arange(rows, dtype=jnp.int32)
    utter_hit = (position[:, None] >= ends[None, :]).astype(jnp.int32)
    utter = jnp.sum(utter_hit, 1)
    onehot = (utter[:, None] == jnp.arange(lengths.shape[0], dtype=jnp.int32)[None, :]).astype(
        jnp.int32
    )
    tok_len = jnp.sum(onehot * lengths[None, :], 1).astype(jnp.float32)
    weight = 2.0 * rows / (tok_len + rows)
    current = (cotangent.astype(jnp.float32) * weight[:, None]).astype(jnp.bfloat16)
    xf = x_saved[0].astype(jnp.float32)
    mean_input = jnp.mean(xf, -1, keepdims=True)
    centered_input = xf - mean_input
    variance = jnp.mean(centered_input * centered_input, -1, keepdims=True)
    inverse_deviation = lax.rsqrt(variance + 1e-05)
    standardized_input = centered_input * inverse_deviation
    gain_vector = gains[0]
    normalized_input = (standardized_input * gain_vector).astype(jnp.bfloat16)
    local = jnp.concatenate([w_in[0], w_out[0].T], axis=1)
    weights = lax.all_gather(local, DP, axis=0, tiled=True)

    inverse_rows = jnp.broadcast_to(inverse_deviation, (rows, 128))
    mean_rows = jnp.broadcast_to(mean_input, (rows, 128))
    gain_row = gain_vector[None, :]
    segments = lax.axis_size("segment")
    my_segment = lax.axis_index("segment")
    first = segments - 1
    slope = lax.cond(
        my_segment == first,
        lambda: jnp.zeros((rows, weights.shape[1] // 2), jnp.bfloat16),
        lambda: hidden_slope(normalized_input, weights),
    )

    def keep(grad_in, kept, kept_gain):
        return kept, kept_gain

    result = current
    gain_local = jnp.zeros((1, width), jnp.float32)
    for level in range(first, -1, -1):
        if level == first:
            def mine(grad_in, kept, kept_gain):
                return fused_back(
                    x_saved[0], grad_in, mean_rows, inverse_rows, gain_row, weights
                )
        else:
            def mine(grad_in, kept, kept_gain):
                return segment_back(
                    grad_in, slope, x_saved[0], mean_rows, inverse_rows, gain_row, weights
                )
        result, gain_local = lax.cond(
            my_segment == level, mine, keep, current, result, gain_local
        )
        if level > 0:
            current = lax.ppermute(result, "segment", [(level, level - 1)])
    gain_total = lax.psum(lax.psum(lax.psum(gain_local, "core"), "y"), "z")
    return (result[None], gain_total)


def solution(mesh):
    n_seg, n_dp = mesh.devices.shape
    shape = (n_seg, n_dp // 8, 4, 2)
    mesh = Mesh(np.asarray(mesh.devices).reshape(shape), ("segment",) + DP)
    in_specs = (
        P("segment", DP, None),
        P("segment", None),
        P("segment", DP, None),
        P("segment", None, DP),
        P(DP, None),
        P(),
    )
    out_specs = (P("segment", DP, None), P("segment", None))
    return jax.shard_map(
        on_device, mesh=mesh, in_specs=in_specs, out_specs=out_specs, check_vma=False
    )
```

```python
import jax
import jax.numpy as jnp
import numpy as np
from jax import lax
from jax.experimental import pallas as pl
from jax.experimental.pallas import tpu as pltpu
from jax.sharding import Mesh, PartitionSpec as P

DP = ("z", "y", "core")
CHUNK = 768


def act_kernel(z_ref, w1_ref, act_ref):
    hidden = jnp.dot(z_ref[...], w1_ref[...], preferred_element_type=jnp.float32)
    sig = jax.nn.sigmoid(hidden)
    act_ref[...] = (sig + hidden * sig * (1.0 - sig)).astype(act_ref.dtype)


def hidden_slope(normed, weights):
    rows, width = normed.shape
    ff = weights.shape[2]
    return pl.pallas_call(
        act_kernel,
        grid=(ff // CHUNK,),
        in_specs=[
            pl.BlockSpec((rows, width), lambda k: (0, 0)),
            pl.BlockSpec((None, width, CHUNK), lambda k: (0, 0, k)),
        ],
        out_specs=pl.BlockSpec((rows, CHUNK), lambda k: (0, k)),
        out_shape=jax.ShapeDtypeStruct((rows, ff), jnp.bfloat16),
        cost_estimate=pl.CostEstimate(
            flops=2 * rows * width * ff, transcendentals=rows * ff,
            bytes_accessed=2 * width * ff + 2 * rows * ff + 2 * rows * width,
        ),
    )(normed, weights)


def fused_kernel(z_ref, g_ref, xh_ref, inv_ref, gain_ref, w1_ref, w2_ref, out_ref, gp_ref, acc_ref):
    k = pl.program_id(0)

    @pl.when(k == 0)
    def _():
        acc_ref[...] = jnp.zeros_like(acc_ref)

    w1 = w1_ref[...]
    hidden = jnp.dot(z_ref[...], w1, preferred_element_type=jnp.float32)
    up_grad = jnp.dot(g_ref[...], w2_ref[...], preferred_element_type=jnp.float32)
    sig = jax.nn.sigmoid(hidden)
    hid_grad = (0.5 * up_grad * (sig + hidden * sig * (1.0 - sig))).astype(jnp.bfloat16)
    acc_ref[...] += lax.dot_general(
        hid_grad, w1, (((1,), (1,)), ((), ())), preferred_element_type=jnp.float32
    )

    @pl.when(k == pl.num_programs(0) - 1)
    def _():
        norm_backward(acc_ref, xh_ref, inv_ref, gain_ref, g_ref, out_ref, gp_ref)


def norm_backward(acc_ref, xh_ref, inv_ref, gain_ref, g_ref, out_ref, gp_ref):
    norm_gradient = acc_ref[...]
    standardized = xh_ref[...]
    gp_ref[...] = jnp.sum(norm_gradient * standardized, axis=0, keepdims=True)
    gain_scaled = norm_gradient * gain_ref[...]
    mean_e = jnp.mean(gain_scaled, axis=-1, keepdims=True)
    mean_ex = jnp.mean(gain_scaled * standardized, axis=-1, keepdims=True)
    back = inv_ref[:, 0:1] * (gain_scaled - mean_e - standardized * mean_ex)
    out_ref[...] = (g_ref[...].astype(jnp.float32) + back).astype(out_ref.dtype)


def fused_back(normed, grad_in, standardized, inverse_deviation, gain_row, weights):
    rows, width = normed.shape
    steps = weights.shape[2] // CHUNK
    whole = lambda k: (0, 0)
    return pl.pallas_call(
        fused_kernel,
        grid=(steps,),
        in_specs=[
            pl.BlockSpec((rows, width), whole),
            pl.BlockSpec((rows, width), whole),
            pl.BlockSpec((rows, width), whole),
            pl.BlockSpec(inverse_deviation.shape, whole),
            pl.BlockSpec((1, width), whole),
            pl.BlockSpec((None, width, CHUNK), lambda k: (0, 0, k)),
            pl.BlockSpec((None, width, CHUNK), lambda k: (1, 0, k)),
        ],
        out_specs=[pl.BlockSpec((rows, width), whole), pl.BlockSpec((1, width), whole)],
        out_shape=[
            jax.ShapeDtypeStruct((rows, width), jnp.bfloat16),
            jax.ShapeDtypeStruct((1, width), jnp.float32),
        ],
        scratch_shapes=[pltpu.VMEM((rows, width), jnp.float32)],
        cost_estimate=pl.CostEstimate(
            flops=6 * rows * width * weights.shape[2],
            transcendentals=rows * weights.shape[2],
            bytes_accessed=2 * weights.size + 12 * rows * width,
        ),
    )(normed, grad_in, standardized, inverse_deviation, gain_row, weights, weights)


def segment_kernel(g_ref, act_ref, xh_ref, inv_ref, gain_ref, w1_ref, w2_ref, out_ref, gp_ref, acc_ref):
    k = pl.program_id(0)

    @pl.when(k == 0)
    def _():
        acc_ref[...] = jnp.zeros_like(acc_ref)

    up_grad = jnp.dot(g_ref[...], w2_ref[...], preferred_element_type=jnp.float32)
    hid_grad = (0.5 * up_grad * act_ref[...].astype(jnp.float32)).astype(jnp.bfloat16)
    acc_ref[...] += lax.dot_general(
        hid_grad, w1_ref[...], (((1,), (1,)), ((), ())), preferred_element_type=jnp.float32
    )

    @pl.when(k == pl.num_programs(0) - 1)
    def _():
        norm_backward(acc_ref, xh_ref, inv_ref, gain_ref, g_ref, out_ref, gp_ref)


def segment_back(grad_in, slope, standardized, inverse_deviation, gain_row, weights):
    rows, width = grad_in.shape
    steps = weights.shape[2] // CHUNK
    whole = lambda k: (0, 0)
    return pl.pallas_call(
        segment_kernel,
        grid=(steps,),
        in_specs=[
            pl.BlockSpec((rows, width), whole),
            pl.BlockSpec((rows, CHUNK), lambda k: (0, k)),
            pl.BlockSpec((rows, width), whole),
            pl.BlockSpec(inverse_deviation.shape, whole),
            pl.BlockSpec((1, width), whole),
            pl.BlockSpec((None, width, CHUNK), lambda k: (0, 0, k)),
            pl.BlockSpec((None, width, CHUNK), lambda k: (1, 0, k)),
        ],
        out_specs=[pl.BlockSpec((rows, width), whole), pl.BlockSpec((1, width), whole)],
        out_shape=[
            jax.ShapeDtypeStruct((rows, width), jnp.bfloat16),
            jax.ShapeDtypeStruct((1, width), jnp.float32),
        ],
        scratch_shapes=[pltpu.VMEM((rows, width), jnp.float32)],
        cost_estimate=pl.CostEstimate(
            flops=4 * rows * width * weights.shape[2],
            transcendentals=0,
            bytes_accessed=2 * weights.size + 2 * rows * weights.shape[1] + 12 * rows * width,
        ),
    )(grad_in, slope, standardized, inverse_deviation, gain_row, weights, weights)


def on_device(x_saved, gains, w_in, w_out, cotangent, lengths):
    rows = cotangent.shape[0]
    width = cotangent.shape[1]
    ends = jnp.cumsum(lengths)
    position = lax.axis_index(DP) * rows + jnp.arange(rows, dtype=jnp.int32)
    utter_hit = (position[:, None] >= ends[None, :]).astype(jnp.int32)
    utter = jnp.sum(utter_hit, 1)
    onehot = (utter[:, None] == jnp.arange(lengths.shape[0], dtype=jnp.int32)[None, :]).astype(
        jnp.int32
    )
    tok_len = jnp.sum(onehot * lengths[None, :], 1).astype(jnp.float32)
    weight = 2.0 * rows / (tok_len + rows)
    current = (cotangent.astype(jnp.float32) * weight[:, None]).astype(jnp.bfloat16)
    xf = x_saved[0].astype(jnp.float32)
    centered_input = xf - jnp.mean(xf, -1, keepdims=True)
    variance = jnp.mean(centered_input * centered_input, -1, keepdims=True)
    inverse_deviation = lax.rsqrt(variance + 1e-05)
    standardized_input = centered_input * inverse_deviation
    gain_vector = gains[0]
    normalized_input = (standardized_input * gain_vector).astype(jnp.bfloat16)
    local = jnp.stack([w_in[0], w_out[0].T])
    weights = lax.all_gather(local, DP, axis=1, tiled=True)

    inverse_rows = jnp.broadcast_to(inverse_deviation, (rows, 128))
    gain_row = gain_vector[None, :]
    segments = lax.axis_size("segment")
    my_segment = lax.axis_index("segment")
    first = segments - 1
    slope = lax.cond(
        my_segment == first,
        lambda: jnp.zeros((rows, weights.shape[2]), jnp.bfloat16),
        lambda: hidden_slope(normalized_input, weights),
    )

    def keep(grad_in, kept, kept_gain):
        return kept, kept_gain

    result = current
    gain_local = jnp.zeros((1, width), jnp.float32)
    for level in range(first, -1, -1):
        if level == first:
            def mine(grad_in, kept, kept_gain):
                return fused_back(
                    normalized_input, grad_in, standardized_input, inverse_rows, gain_row, weights
                )
        else:
            def mine(grad_in, kept, kept_gain):
                return segment_back(
                    grad_in, slope, standardized_input, inverse_rows, gain_row, weights
                )
        result, gain_local = lax.cond(
            my_segment == level, mine, keep, current, result, gain_local
        )
        if level > 0:
            current = lax.ppermute(result, "segment", [(level, level - 1)])
    gain_total = lax.psum(lax.psum(lax.psum(gain_local, "core"), "y"), "z")
    return (result[None], gain_total)


def solution(mesh):
    n_seg, n_dp = mesh.devices.shape
    shape = (n_seg, n_dp // 8, 4, 2)
    mesh = Mesh(np.asarray(mesh.devices).reshape(shape), ("segment",) + DP)
    in_specs = (
        P("segment", DP, None),
        P("segment", None),
        P("segment", DP, None),
        P("segment", None, DP),
        P(DP, None),
        P(),
    )
    out_specs = (P("segment", DP, None), P("segment", None))
    return jax.shard_map(
        on_device, mesh=mesh, in_specs=in_specs, out_specs=out_specs, check_vma=False
    )
```

```python
import jax
import jax.numpy as jnp
import numpy as np
from jax import lax
from jax.experimental import pallas as pl
from jax.experimental.pallas import tpu as pltpu
from jax.sharding import Mesh, PartitionSpec as P

DP = ("z", "y", "core")
CHUNK = 768


def act_kernel(z_ref, w1_ref, act_ref):
    hidden = jnp.dot(z_ref[...], w1_ref[...], preferred_element_type=jnp.float32)
    sig = jax.nn.sigmoid(hidden)
    act_ref[...] = (sig + hidden * sig * (1.0 - sig)).astype(act_ref.dtype)


def hidden_slope(normed, weights):
    rows, width = normed.shape
    ff = weights.shape[1] // 2
    return pl.pallas_call(
        act_kernel,
        grid=(ff // CHUNK,),
        in_specs=[
            pl.BlockSpec((rows, width), lambda k: (0, 0)),
            pl.BlockSpec((width, CHUNK), lambda k: (0, k)),
        ],
        out_specs=pl.BlockSpec((rows, CHUNK), lambda k: (0, k)),
        out_shape=jax.ShapeDtypeStruct((rows, ff), jnp.bfloat16),
        cost_estimate=pl.CostEstimate(
            flops=2 * rows * width * ff, transcendentals=rows * ff,
            bytes_accessed=2 * width * ff + 2 * rows * ff + 2 * rows * width,
        ),
    )(normed, weights)


def fused_kernel(z_ref, g_ref, xh_ref, inv_ref, gain_ref, w1_ref, w2_ref, out_ref, gp_ref, acc_ref):
    k = pl.program_id(0)

    @pl.when(k == 0)
    def _():
        acc_ref[...] = jnp.zeros_like(acc_ref)

    w1 = w1_ref[...]
    hidden = jnp.dot(z_ref[...], w1, preferred_element_type=jnp.float32)
    up_grad = jnp.dot(g_ref[...], w2_ref[...], preferred_element_type=jnp.float32)
    sig = jax.nn.sigmoid(hidden)
    hid_grad = (0.5 * up_grad * (sig + hidden * sig * (1.0 - sig))).astype(jnp.bfloat16)
    acc_ref[...] += lax.dot_general(
        hid_grad, w1, (((1,), (1,)), ((), ())), preferred_element_type=jnp.float32
    )

    @pl.when(k == pl.num_programs(0) - 1)
    def _():
        norm_backward(acc_ref, xh_ref, inv_ref, gain_ref, g_ref, out_ref, gp_ref)


def norm_backward(acc_ref, xh_ref, inv_ref, gain_ref, g_ref, out_ref, gp_ref):
    norm_gradient = acc_ref[...]
    standardized = xh_ref[...]
    gp_ref[...] = jnp.sum(norm_gradient * standardized, axis=0, keepdims=True)
    gain_scaled = norm_gradient * gain_ref[...]
    mean_e = jnp.mean(gain_scaled, axis=-1, keepdims=True)
    mean_ex = jnp.mean(gain_scaled * standardized, axis=-1, keepdims=True)
    back = inv_ref[:, 0:1] * (gain_scaled - mean_e - standardized * mean_ex)
    out_ref[...] = (g_ref[...].astype(jnp.float32) + back).astype(out_ref.dtype)


def fused_back(normed, grad_in, standardized, inverse_deviation, gain_row, weights):
    rows, width = normed.shape
    steps = weights.shape[1] // 2 // CHUNK
    whole = lambda k: (0, 0)
    return pl.pallas_call(
        fused_kernel,
        grid=(steps,),
        in_specs=[
            pl.BlockSpec((rows, width), whole),
            pl.BlockSpec((rows, width), whole),
            pl.BlockSpec((rows, width), whole),
            pl.BlockSpec(inverse_deviation.shape, whole),
            pl.BlockSpec((1, width), whole),
            pl.BlockSpec((width, CHUNK), lambda k: (0, k)),
            pl.BlockSpec((width, CHUNK), lambda k: (0, k + steps)),
        ],
        out_specs=[pl.BlockSpec((rows, width), whole), pl.BlockSpec((1, width), whole)],
        out_shape=[
            jax.ShapeDtypeStruct((rows, width), jnp.bfloat16),
            jax.ShapeDtypeStruct((1, width), jnp.float32),
        ],
        scratch_shapes=[pltpu.VMEM((rows, width), jnp.float32)],
        cost_estimate=pl.CostEstimate(
            flops=6 * rows * width * weights.shape[1] // 2,
            transcendentals=rows * weights.shape[1] // 2,
            bytes_accessed=2 * weights.size + 12 * rows * width,
        ),
    )(normed, grad_in, standardized, inverse_deviation, gain_row, weights, weights)


def segment_kernel(g_ref, act_ref, xh_ref, inv_ref, gain_ref, w1_ref, w2_ref, out_ref, gp_ref, acc_ref):
    k = pl.program_id(0)

    @pl.when(k == 0)
    def _():
        acc_ref[...] = jnp.zeros_like(acc_ref)

    up_grad = jnp.dot(g_ref[...], w2_ref[...], preferred_element_type=jnp.float32)
    hid_grad = (0.5 * up_grad * act_ref[...].astype(jnp.float32)).astype(jnp.bfloat16)
    acc_ref[...] += lax.dot_general(
        hid_grad, w1_ref[...], (((1,), (1,)), ((), ())), preferred_element_type=jnp.float32
    )

    @pl.when(k == pl.num_programs(0) - 1)
    def _():
        norm_backward(acc_ref, xh_ref, inv_ref, gain_ref, g_ref, out_ref, gp_ref)


def segment_back(grad_in, slope, standardized, inverse_deviation, gain_row, weights):
    rows, width = grad_in.shape
    steps = weights.shape[1] // 2 // CHUNK
    whole = lambda k: (0, 0)
    return pl.pallas_call(
        segment_kernel,
        grid=(steps,),
        in_specs=[
            pl.BlockSpec((rows, width), whole),
            pl.BlockSpec((rows, CHUNK), lambda k: (0, k)),
            pl.BlockSpec((rows, width), whole),
            pl.BlockSpec(inverse_deviation.shape, whole),
            pl.BlockSpec((1, width), whole),
            pl.BlockSpec((width, CHUNK), lambda k: (0, k)),
            pl.BlockSpec((width, CHUNK), lambda k: (0, k + steps)),
        ],
        out_specs=[pl.BlockSpec((rows, width), whole), pl.BlockSpec((1, width), whole)],
        out_shape=[
            jax.ShapeDtypeStruct((rows, width), jnp.bfloat16),
            jax.ShapeDtypeStruct((1, width), jnp.float32),
        ],
        scratch_shapes=[pltpu.VMEM((rows, width), jnp.float32)],
        cost_estimate=pl.CostEstimate(
            flops=4 * rows * width * weights.shape[1] // 2,
            transcendentals=0,
            bytes_accessed=2 * weights.size + 2 * rows * weights.shape[1] + 12 * rows * width,
        ),
    )(grad_in, slope, standardized, inverse_deviation, gain_row, weights, weights)


def on_device(x_saved, gains, w_in, w_out, cotangent, lengths):
    rows = cotangent.shape[0]
    width = cotangent.shape[1]
    ends = jnp.cumsum(lengths)
    position = lax.axis_index(DP) * rows + jnp.arange(rows, dtype=jnp.int32)
    utter_hit = (position[:, None] >= ends[None, :]).astype(jnp.int32)
    utter = jnp.sum(utter_hit, 1)
    onehot = (utter[:, None] == jnp.arange(lengths.shape[0], dtype=jnp.int32)[None, :]).astype(
        jnp.int32
    )
    tok_len = jnp.sum(onehot * lengths[None, :], 1).astype(jnp.float32)
    weight = 2.0 * rows / (tok_len + rows)
    current = (cotangent.astype(jnp.float32) * weight[:, None]).astype(jnp.bfloat16)
    xf = x_saved[0].astype(jnp.float32)
    centered_input = xf - jnp.mean(xf, -1, keepdims=True)
    variance = jnp.mean(centered_input * centered_input, -1, keepdims=True)
    inverse_deviation = lax.rsqrt(variance + 1e-05)
    standardized_input = centered_input * inverse_deviation
    gain_vector = gains[0]
    normalized_input = (standardized_input * gain_vector).astype(jnp.bfloat16)
    local = jnp.concatenate([w_in[0], w_out[0].T], axis=1)
    weights = lax.all_gather(local, DP, axis=0, tiled=True)

    inverse_rows = jnp.broadcast_to(inverse_deviation, (rows, 128))
    gain_row = gain_vector[None, :]
    segments = lax.axis_size("segment")
    my_segment = lax.axis_index("segment")
    first = segments - 1
    slope = lax.cond(
        my_segment == first,
        lambda: jnp.zeros((rows, weights.shape[1] // 2), jnp.bfloat16),
        lambda: hidden_slope(normalized_input, weights),
    )

    def keep(grad_in, kept, kept_gain):
        return kept, kept_gain

    result = current
    gain_local = jnp.zeros((1, width), jnp.float32)
    for level in range(first, -1, -1):
        if level == first:
            def mine(grad_in, kept, kept_gain):
                return fused_back(
                    normalized_input, grad_in, standardized_input, inverse_rows, gain_row, weights
                )
        else:
            def mine(grad_in, kept, kept_gain):
                return segment_back(
                    grad_in, slope, standardized_input, inverse_rows, gain_row, weights
                )
        result, gain_local = lax.cond(
            my_segment == level, mine, keep, current, result, gain_local
        )
        if level > 0:
            current = lax.ppermute(result, "segment", [(level, level - 1)])
    dense = gain_local.reshape(width // 128, 128)
    gain_total = lax.psum(lax.psum(lax.psum(dense, "core"), "y"), "z").reshape(1, width)
    return (result[None], gain_total)


def solution(mesh):
    n_seg, n_dp = mesh.devices.shape
    shape = (n_seg, n_dp // 8, 4, 2)
    mesh = Mesh(np.asarray(mesh.devices).reshape(shape), ("segment",) + DP)
    in_specs = (
        P("segment", DP, None),
        P("segment", None),
        P("segment", DP, None),
        P("segment", None, DP),
        P(DP, None),
        P(),
    )
    out_specs = (P("segment", DP, None), P("segment", None))
    return jax.shard_map(
        on_device, mesh=mesh, in_specs=in_specs, out_specs=out_specs, check_vma=False
    )
```

```python
import jax
import jax.numpy as jnp
import numpy as np
from jax import lax
from jax.experimental import pallas as pl
from jax.experimental.pallas import tpu as pltpu
from jax.sharding import Mesh, PartitionSpec as P

DP = ("z", "y", "core")
CHUNK = 768


def act_kernel(z_ref, w1_ref, act_ref):
    hidden = jnp.dot(z_ref[...], w1_ref[...], preferred_element_type=jnp.float32)
    sig = jax.nn.sigmoid(hidden)
    act_ref[...] = (sig + hidden * sig * (1.0 - sig)).astype(act_ref.dtype)


def hidden_slope(normed, weights):
    rows, width = normed.shape
    ff = weights.shape[1] // 2
    return pl.pallas_call(
        act_kernel,
        grid=(ff // CHUNK,),
        in_specs=[
            pl.BlockSpec((rows, width), lambda k: (0, 0)),
            pl.BlockSpec((width, CHUNK), lambda k: (0, k)),
        ],
        out_specs=pl.BlockSpec((rows, CHUNK), lambda k: (0, k)),
        out_shape=jax.ShapeDtypeStruct((rows, ff), jnp.bfloat16),
        cost_estimate=pl.CostEstimate(
            flops=2 * rows * width * ff, transcendentals=rows * ff,
            bytes_accessed=2 * width * ff + 2 * rows * ff + 2 * rows * width,
        ),
    )(normed, weights)


def fused_kernel(z_ref, g_ref, xh_ref, inv_ref, gain_ref, w1_ref, w2_ref, out_ref, gp_ref, acc_ref):
    k = pl.program_id(0)

    @pl.when(k == 0)
    def _():
        acc_ref[...] = jnp.zeros_like(acc_ref)

    w1 = w1_ref[...]
    hidden = jnp.dot(z_ref[...], w1, preferred_element_type=jnp.float32)
    up_grad = jnp.dot(g_ref[...], w2_ref[...], preferred_element_type=jnp.float32)
    sig = jax.nn.sigmoid(hidden)
    hid_grad = (0.5 * up_grad * (sig + hidden * sig * (1.0 - sig))).astype(jnp.bfloat16)
    acc_ref[...] += lax.dot_general(
        hid_grad, w1, (((1,), (1,)), ((), ())), preferred_element_type=jnp.float32
    )

    @pl.when(k == pl.num_programs(0) - 1)
    def _():
        norm_backward(acc_ref, xh_ref, inv_ref, gain_ref, g_ref, out_ref, gp_ref)


def norm_backward(acc_ref, xh_ref, inv_ref, gain_ref, g_ref, out_ref, gp_ref):
    norm_gradient = acc_ref[...]
    standardized = xh_ref[...]
    gp_ref[...] = jnp.sum(norm_gradient * standardized, axis=0, keepdims=True)
    gain_scaled = norm_gradient * gain_ref[...]
    mean_e = jnp.mean(gain_scaled, axis=-1, keepdims=True)
    mean_ex = jnp.mean(gain_scaled * standardized, axis=-1, keepdims=True)
    back = inv_ref[:, 0:1] * (gain_scaled - mean_e - standardized * mean_ex)
    out_ref[...] = (g_ref[...].astype(jnp.float32) + back).astype(out_ref.dtype)


def fused_back(normed, grad_in, standardized, inverse_deviation, gain_row, weights):
    rows, width = normed.shape
    steps = weights.shape[1] // 2 // CHUNK
    whole = lambda k: (0, 0)
    return pl.pallas_call(
        fused_kernel,
        grid=(steps,),
        in_specs=[
            pl.BlockSpec((rows, width), whole),
            pl.BlockSpec((rows, width), whole),
            pl.BlockSpec((rows, width), whole),
            pl.BlockSpec(inverse_deviation.shape, whole),
            pl.BlockSpec((1, width), whole),
            pl.BlockSpec((width, CHUNK), lambda k: (0, k)),
            pl.BlockSpec((width, CHUNK), lambda k: (0, k + steps)),
        ],
        out_specs=[pl.BlockSpec((rows, width), whole), pl.BlockSpec((1, width), whole)],
        out_shape=[
            jax.ShapeDtypeStruct((rows, width), jnp.bfloat16),
            jax.ShapeDtypeStruct((1, width), jnp.float32),
        ],
        scratch_shapes=[pltpu.VMEM((rows, width), jnp.float32)],
        cost_estimate=pl.CostEstimate(
            flops=6 * rows * width * weights.shape[1] // 2,
            transcendentals=rows * weights.shape[1] // 2,
            bytes_accessed=2 * weights.size + 12 * rows * width,
        ),
    )(normed, grad_in, standardized, inverse_deviation, gain_row, weights, weights)


def segment_kernel(g_ref, act_ref, xh_ref, inv_ref, gain_ref, w1_ref, w2_ref, out_ref, gp_ref, acc_ref):
    k = pl.program_id(0)

    @pl.when(k == 0)
    def _():
        acc_ref[...] = jnp.zeros_like(acc_ref)

    up_grad = jnp.dot(g_ref[...], w2_ref[...], preferred_element_type=jnp.float32)
    hid_grad = (0.5 * up_grad * act_ref[...].astype(jnp.float32)).astype(jnp.bfloat16)
    acc_ref[...] += lax.dot_general(
        hid_grad, w1_ref[...], (((1,), (1,)), ((), ())), preferred_element_type=jnp.float32
    )

    @pl.when(k == pl.num_programs(0) - 1)
    def _():
        norm_backward(acc_ref, xh_ref, inv_ref, gain_ref, g_ref, out_ref, gp_ref)


def segment_back(grad_in, slope, standardized, inverse_deviation, gain_row, weights):
    rows, width = grad_in.shape
    steps = weights.shape[1] // 2 // CHUNK
    whole = lambda k: (0, 0)
    return pl.pallas_call(
        segment_kernel,
        grid=(steps,),
        in_specs=[
            pl.BlockSpec((rows, width), whole),
            pl.BlockSpec((rows, CHUNK), lambda k: (0, k)),
            pl.BlockSpec((rows, width), whole),
            pl.BlockSpec(inverse_deviation.shape, whole),
            pl.BlockSpec((1, width), whole),
            pl.BlockSpec((width, CHUNK), lambda k: (0, k)),
            pl.BlockSpec((width, CHUNK), lambda k: (0, k + steps)),
        ],
        out_specs=[pl.BlockSpec((rows, width), whole), pl.BlockSpec((1, width), whole)],
        out_shape=[
            jax.ShapeDtypeStruct((rows, width), jnp.bfloat16),
            jax.ShapeDtypeStruct((1, width), jnp.float32),
        ],
        scratch_shapes=[pltpu.VMEM((rows, width), jnp.float32)],
        cost_estimate=pl.CostEstimate(
            flops=4 * rows * width * weights.shape[1] // 2,
            transcendentals=0,
            bytes_accessed=2 * weights.size + 2 * rows * weights.shape[1] + 12 * rows * width,
        ),
    )(grad_in, slope, standardized, inverse_deviation, gain_row, weights, weights)


def on_device(x_saved, gains, w_in, w_out, cotangent, lengths):
    rows = cotangent.shape[0]
    width = cotangent.shape[1]
    ends = jnp.cumsum(lengths)
    position = lax.axis_index(DP) * rows + jnp.arange(rows, dtype=jnp.int32)
    utter_hit = (position[:, None] >= ends[None, :]).astype(jnp.int32)
    utter = jnp.sum(utter_hit, 1)
    onehot = (utter[:, None] == jnp.arange(lengths.shape[0], dtype=jnp.int32)[None, :]).astype(
        jnp.int32
    )
    tok_len = jnp.sum(onehot * lengths[None, :], 1).astype(jnp.float32)
    weight = 2.0 * rows / (tok_len + rows)
    current = (cotangent.astype(jnp.float32) * weight[:, None]).astype(jnp.bfloat16)
    xf = x_saved[0].astype(jnp.float32)
    centered_input = xf - jnp.mean(xf, -1, keepdims=True)
    variance = jnp.mean(centered_input * centered_input, -1, keepdims=True)
    inverse_deviation = lax.rsqrt(variance + 1e-05)
    standardized_input = centered_input * inverse_deviation
    gain_vector = gains[0]
    normalized_input = (standardized_input * gain_vector).astype(jnp.bfloat16)
    local = jnp.concatenate([w_in[0], w_out[0].T], axis=1)
    weights = lax.all_gather(local, DP, axis=0, tiled=True)

    inverse_rows = jnp.broadcast_to(inverse_deviation, (rows, 128))
    gain_row = gain_vector[None, :]
    segments = lax.axis_size("segment")
    my_segment = lax.axis_index("segment")
    first = segments - 1
    slope = lax.cond(
        my_segment == first,
        lambda: jnp.zeros((rows, weights.shape[1] // 2), jnp.bfloat16),
        lambda: hidden_slope(normalized_input, weights),
    )

    def keep(grad_in, kept, kept_gain):
        return kept, kept_gain

    result = current
    gain_local = jnp.zeros((1, width), jnp.float32)
    for level in range(first, -1, -1):
        if level == first:
            def mine(grad_in, kept, kept_gain):
                return fused_back(
                    normalized_input, grad_in, standardized_input, inverse_rows, gain_row, weights
                )
        else:
            def mine(grad_in, kept, kept_gain):
                return segment_back(
                    grad_in, slope, standardized_input, inverse_rows, gain_row, weights
                )
        result, gain_local = lax.cond(
            my_segment == level, mine, keep, current, result, gain_local
        )
        if level > 0:
            half = rows // 2
            pair = [(level, level - 1)]
            current = jnp.concatenate(
                [
                    lax.ppermute(result[:half], "segment", pair),
                    lax.ppermute(result[half:], "segment", pair),
                ]
            )
    gain_total = lax.psum(lax.psum(lax.psum(gain_local, "core"), "y"), "z")
    return (result[None], gain_total)


def solution(mesh):
    n_seg, n_dp = mesh.devices.shape
    shape = (n_seg, n_dp // 8, 4, 2)
    mesh = Mesh(np.asarray(mesh.devices).reshape(shape), ("segment",) + DP)
    in_specs = (
        P("segment", DP, None),
        P("segment", None),
        P("segment", DP, None),
        P("segment", None, DP),
        P(DP, None),
        P(),
    )
    out_specs = (P("segment", DP, None), P("segment", None))
    return jax.shard_map(
        on_device, mesh=mesh, in_specs=in_specs, out_specs=out_specs, check_vma=False
    )
```

```python
import jax
import jax.numpy as jnp
import numpy as np
from jax import lax
from jax.experimental import pallas as pl
from jax.experimental.pallas import tpu as pltpu
from jax.sharding import Mesh, PartitionSpec as P

DP = ("z", "y", "core")
CHUNK = 768


def act_kernel(z_ref, w1_ref, act_ref):
    hidden = jnp.dot(z_ref[...], w1_ref[...], preferred_element_type=jnp.float32)
    sig = jax.nn.sigmoid(hidden)
    act_ref[...] = (sig + hidden * sig * (1.0 - sig)).astype(act_ref.dtype)


def hidden_slope(normed, weights):
    rows, width = normed.shape
    ff = weights.shape[1] // 2
    return pl.pallas_call(
        act_kernel,
        grid=(ff // CHUNK,),
        in_specs=[
            pl.BlockSpec((rows, width), lambda k: (0, 0)),
            pl.BlockSpec((width, CHUNK), lambda k: (0, k)),
        ],
        out_specs=pl.BlockSpec((rows, CHUNK), lambda k: (0, k)),
        out_shape=jax.ShapeDtypeStruct((rows, ff), jnp.bfloat16),
        cost_estimate=pl.CostEstimate(
            flops=2 * rows * width * ff, transcendentals=rows * ff,
            bytes_accessed=2 * width * ff + 2 * rows * ff + 2 * rows * width,
        ),
    )(normed, weights)


def fused_kernel(z_ref, g_ref, xh_ref, inv_ref, gain_ref, w1_ref, w2_ref, out_ref, gp_ref, acc_ref):
    k = pl.program_id(0)

    @pl.when(k == 0)
    def _():
        acc_ref[...] = jnp.zeros_like(acc_ref)

    w1 = w1_ref[...]
    hidden = jnp.dot(z_ref[...], w1, preferred_element_type=jnp.float32)
    up_grad = jnp.dot(g_ref[...], w2_ref[...], preferred_element_type=jnp.float32)
    sig = jax.nn.sigmoid(hidden)
    hid_grad = (0.5 * up_grad * (sig + hidden * sig * (1.0 - sig))).astype(jnp.bfloat16)
    acc_ref[...] += lax.dot_general(
        hid_grad, w1, (((1,), (1,)), ((), ())), preferred_element_type=jnp.float32
    )

    @pl.when(k == pl.num_programs(0) - 1)
    def _():
        norm_backward(acc_ref, xh_ref, inv_ref, gain_ref, g_ref, out_ref, gp_ref)


def norm_backward(acc_ref, xh_ref, inv_ref, gain_ref, g_ref, out_ref, gp_ref):
    norm_gradient = acc_ref[...]
    standardized = xh_ref[...]
    gp_ref[...] = jnp.sum(norm_gradient * standardized, axis=0, keepdims=True)
    gain_scaled = norm_gradient * gain_ref[...]
    mean_e = jnp.mean(gain_scaled, axis=-1, keepdims=True)
    mean_ex = jnp.mean(gain_scaled * standardized, axis=-1, keepdims=True)
    back = inv_ref[:, 0:1] * (gain_scaled - mean_e - standardized * mean_ex)
    out_ref[...] = (g_ref[...].astype(jnp.float32) + back).astype(out_ref.dtype)


def fused_back(normed, grad_in, standardized, inverse_deviation, gain_row, weights):
    rows, width = normed.shape
    steps = weights.shape[1] // 2 // CHUNK
    whole = lambda k: (0, 0)
    return pl.pallas_call(
        fused_kernel,
        grid=(steps,),
        in_specs=[
            pl.BlockSpec((rows, width), whole),
            pl.BlockSpec((rows, width), whole),
            pl.BlockSpec((rows, width), whole),
            pl.BlockSpec(inverse_deviation.shape, whole),
            pl.BlockSpec((1, width), whole),
            pl.BlockSpec((width, CHUNK), lambda k: (0, k)),
            pl.BlockSpec((width, CHUNK), lambda k: (0, k + steps)),
        ],
        out_specs=[pl.BlockSpec((rows, width), whole), pl.BlockSpec((1, width), whole)],
        out_shape=[
            jax.ShapeDtypeStruct((rows, width), jnp.bfloat16),
            jax.ShapeDtypeStruct((1, width), jnp.float32),
        ],
        scratch_shapes=[pltpu.VMEM((rows, width), jnp.float32)],
        cost_estimate=pl.CostEstimate(
            flops=6 * rows * width * weights.shape[1] // 2,
            transcendentals=rows * weights.shape[1] // 2,
            bytes_accessed=2 * weights.size + 12 * rows * width,
        ),
    )(normed, grad_in, standardized, inverse_deviation, gain_row, weights, weights)


def segment_kernel(g_ref, act_ref, xh_ref, inv_ref, gain_ref, w1_ref, w2_ref, out_ref, gp_ref, acc_ref):
    k = pl.program_id(0)

    @pl.when(k == 0)
    def _():
        acc_ref[...] = jnp.zeros_like(acc_ref)

    up_grad = jnp.dot(g_ref[...], w2_ref[...], preferred_element_type=jnp.float32)
    hid_grad = (0.5 * up_grad * act_ref[...].astype(jnp.float32)).astype(jnp.bfloat16)
    acc_ref[...] += lax.dot_general(
        hid_grad, w1_ref[...], (((1,), (1,)), ((), ())), preferred_element_type=jnp.float32
    )

    @pl.when(k == pl.num_programs(0) - 1)
    def _():
        norm_backward(acc_ref, xh_ref, inv_ref, gain_ref, g_ref, out_ref, gp_ref)


def segment_back(grad_in, slope, standardized, inverse_deviation, gain_row, weights):
    rows, width = grad_in.shape
    steps = weights.shape[1] // 2 // CHUNK
    whole = lambda k: (0, 0)
    return pl.pallas_call(
        segment_kernel,
        grid=(steps,),
        in_specs=[
            pl.BlockSpec((rows, width), whole),
            pl.BlockSpec((rows, CHUNK), lambda k: (0, k)),
            pl.BlockSpec((rows, width), whole),
            pl.BlockSpec(inverse_deviation.shape, whole),
            pl.BlockSpec((1, width), whole),
            pl.BlockSpec((width, CHUNK), lambda k: (0, k)),
            pl.BlockSpec((width, CHUNK), lambda k: (0, k + steps)),
        ],
        out_specs=[pl.BlockSpec((rows, width), whole), pl.BlockSpec((1, width), whole)],
        out_shape=[
            jax.ShapeDtypeStruct((rows, width), jnp.bfloat16),
            jax.ShapeDtypeStruct((1, width), jnp.float32),
        ],
        scratch_shapes=[pltpu.VMEM((rows, width), jnp.float32)],
        cost_estimate=pl.CostEstimate(
            flops=4 * rows * width * weights.shape[1] // 2,
            transcendentals=0,
            bytes_accessed=2 * weights.size + 2 * rows * weights.shape[1] + 12 * rows * width,
        ),
    )(grad_in, slope, standardized, inverse_deviation, gain_row, weights, weights)


def on_device(x_saved, gains, w_in, w_out, cotangent, lengths):
    rows = cotangent.shape[0]
    width = cotangent.shape[1]
    ends = jnp.cumsum(lengths)
    position = lax.axis_index(DP) * rows + jnp.arange(rows, dtype=jnp.int32)
    utter_hit = (position[:, None] >= ends[None, :]).astype(jnp.int32)
    utter = jnp.sum(utter_hit, 1)
    onehot = (utter[:, None] == jnp.arange(lengths.shape[0], dtype=jnp.int32)[None, :]).astype(
        jnp.int32
    )
    tok_len = jnp.sum(onehot * lengths[None, :], 1).astype(jnp.float32)
    weight = 2.0 * rows / (tok_len + rows)
    current = (cotangent.astype(jnp.float32) * weight[:, None]).astype(jnp.bfloat16)
    xf = x_saved[0].astype(jnp.float32)
    centered_input = xf - jnp.mean(xf, -1, keepdims=True)
    variance = jnp.mean(centered_input * centered_input, -1, keepdims=True)
    inverse_deviation = lax.rsqrt(variance + 1e-05)
    standardized_input = centered_input * inverse_deviation
    gain_vector = gains[0]
    normalized_input = (standardized_input * gain_vector).astype(jnp.bfloat16)
    local = jnp.concatenate([w_in[0], w_out[0].T], axis=1)
    weights = lax.all_gather(local, DP, axis=0, tiled=True)

    inverse_rows = jnp.broadcast_to(inverse_deviation, (rows, 128))
    gain_row = gain_vector[None, :]
    segments = lax.axis_size("segment")
    my_segment = lax.axis_index("segment")
    first = segments - 1
    slope = lax.cond(
        my_segment == first,
        lambda: jnp.zeros((rows, weights.shape[1] // 2), jnp.bfloat16),
        lambda: hidden_slope(normalized_input, weights),
    )

    def keep(grad_in, kept, kept_gain):
        return kept, kept_gain

    result = current
    gain_local = jnp.zeros((1, width), jnp.float32)
    for level in range(first, -1, -1):
        if level == first:
            def mine(grad_in, kept, kept_gain):
                return fused_back(
                    normalized_input, grad_in, standardized_input, inverse_rows, gain_row, weights
                )
        else:
            def mine(grad_in, kept, kept_gain):
                return segment_back(
                    grad_in, slope, standardized_input, inverse_rows, gain_row, weights
                )
        result, gain_local = lax.cond(
            my_segment == level, mine, keep, current, result, gain_local
        )
        if level > 0:
            current = lax.ppermute(result, "segment", [(level, level - 1)])
    pair_sum = gain_local + lax.ppermute(gain_local, "core", [(0, 1), (1, 0)])
    gain_total = lax.psum(lax.psum(pair_sum, "y"), "z")
    return (result[None], gain_total)


def solution(mesh):
    n_seg, n_dp = mesh.devices.shape
    shape = (n_seg, n_dp // 8, 4, 2)
    mesh = Mesh(np.asarray(mesh.devices).reshape(shape), ("segment",) + DP)
    in_specs = (
        P("segment", DP, None),
        P("segment", None),
        P("segment", DP, None),
        P("segment", None, DP),
        P(DP, None),
        P(),
    )
    out_specs = (P("segment", DP, None), P("segment", None))
    return jax.shard_map(
        on_device, mesh=mesh, in_specs=in_specs, out_specs=out_specs, check_vma=False
    )
```

```python
import jax
import jax.numpy as jnp
import numpy as np
from jax import lax
from jax.experimental import pallas as pl
from jax.experimental.pallas import tpu as pltpu
from jax.sharding import Mesh, PartitionSpec as P

DP = ("z", "y", "core")
CHUNK = 768


def act_kernel(z_ref, w1_ref, act_ref):
    hidden = jnp.dot(z_ref[...], w1_ref[...], preferred_element_type=jnp.float32)
    sig = jax.nn.sigmoid(hidden)
    act_ref[...] = (sig + hidden * sig * (1.0 - sig)).astype(act_ref.dtype)


def hidden_slope(normed, weights):
    rows, width = normed.shape
    ff = weights.shape[1] // 2
    return pl.pallas_call(
        act_kernel,
        grid=(ff // CHUNK,),
        in_specs=[
            pl.BlockSpec((rows, width), lambda k: (0, 0)),
            pl.BlockSpec((width, CHUNK), lambda k: (0, k)),
        ],
        out_specs=pl.BlockSpec((rows, CHUNK), lambda k: (0, k)),
        out_shape=jax.ShapeDtypeStruct((rows, ff), jnp.bfloat16),
        cost_estimate=pl.CostEstimate(
            flops=2 * rows * width * ff, transcendentals=rows * ff,
            bytes_accessed=2 * width * ff + 2 * rows * ff + 2 * rows * width,
        ),
    )(normed, weights)


def fused_kernel(z_ref, g_ref, xh_ref, inv_ref, gain_ref, w1_ref, w2_ref, out_ref, gp_ref, acc_ref):
    k = pl.program_id(0)

    @pl.when(k == 0)
    def _():
        acc_ref[...] = jnp.zeros_like(acc_ref)

    w1 = w1_ref[...]
    hidden = jnp.dot(z_ref[...], w1, preferred_element_type=jnp.float32)
    up_grad = jnp.dot(g_ref[...], w2_ref[...], preferred_element_type=jnp.float32)
    sig = jax.nn.sigmoid(hidden)
    hid_grad = (0.5 * up_grad * (sig + hidden * sig * (1.0 - sig))).astype(jnp.bfloat16)
    acc_ref[...] += lax.dot_general(
        hid_grad, w1, (((1,), (1,)), ((), ())), preferred_element_type=jnp.float32
    )

    @pl.when(k == pl.num_programs(0) - 1)
    def _():
        norm_backward(acc_ref, xh_ref, inv_ref, gain_ref, g_ref, out_ref, gp_ref)


def norm_backward(acc_ref, xh_ref, inv_ref, gain_ref, g_ref, out_ref, gp_ref):
    norm_gradient = acc_ref[...]
    standardized = xh_ref[...]
    gp_ref[...] = jnp.sum(norm_gradient * standardized, axis=0, keepdims=True)
    gain_scaled = norm_gradient * gain_ref[...]
    mean_e = jnp.mean(gain_scaled, axis=-1, keepdims=True)
    mean_ex = jnp.mean(gain_scaled * standardized, axis=-1, keepdims=True)
    back = inv_ref[:, 0:1] * (gain_scaled - mean_e - standardized * mean_ex)
    out_ref[...] = (g_ref[...].astype(jnp.float32) + back).astype(out_ref.dtype)


def fused_back(normed, grad_in, standardized, inverse_deviation, gain_row, weights):
    rows, width = normed.shape
    steps = weights.shape[1] // 2 // CHUNK
    whole = lambda k: (0, 0)
    return pl.pallas_call(
        fused_kernel,
        grid=(steps,),
        in_specs=[
            pl.BlockSpec((rows, width), whole),
            pl.BlockSpec((rows, width), whole),
            pl.BlockSpec((rows, width), whole),
            pl.BlockSpec(inverse_deviation.shape, whole),
            pl.BlockSpec((1, width), whole),
            pl.BlockSpec((width, CHUNK), lambda k: (0, k)),
            pl.BlockSpec((width, CHUNK), lambda k: (0, k + steps)),
        ],
        out_specs=[pl.BlockSpec((rows, width), whole), pl.BlockSpec((1, width), whole)],
        out_shape=[
            jax.ShapeDtypeStruct((rows, width), jnp.bfloat16),
            jax.ShapeDtypeStruct((1, width), jnp.float32),
        ],
        scratch_shapes=[pltpu.VMEM((rows, width), jnp.float32)],
        cost_estimate=pl.CostEstimate(
            flops=6 * rows * width * weights.shape[1] // 2,
            transcendentals=rows * weights.shape[1] // 2,
            bytes_accessed=2 * weights.size + 12 * rows * width,
        ),
    )(normed, grad_in, standardized, inverse_deviation, gain_row, weights, weights)


def segment_kernel(g_ref, act_ref, xh_ref, inv_ref, gain_ref, w1_ref, w2_ref, out_ref, gp_ref, acc_ref):
    k = pl.program_id(0)

    @pl.when(k == 0)
    def _():
        acc_ref[...] = jnp.zeros_like(acc_ref)

    up_grad = jnp.dot(g_ref[...], w2_ref[...], preferred_element_type=jnp.float32)
    hid_grad = (0.5 * up_grad * act_ref[...].astype(jnp.float32)).astype(jnp.bfloat16)
    acc_ref[...] += lax.dot_general(
        hid_grad, w1_ref[...], (((1,), (1,)), ((), ())), preferred_element_type=jnp.float32
    )

    @pl.when(k == pl.num_programs(0) - 1)
    def _():
        norm_backward(acc_ref, xh_ref, inv_ref, gain_ref, g_ref, out_ref, gp_ref)


def segment_back(grad_in, slope, standardized, inverse_deviation, gain_row, weights):
    rows, width = grad_in.shape
    steps = weights.shape[1] // 2 // CHUNK
    whole = lambda k: (0, 0)
    return pl.pallas_call(
        segment_kernel,
        grid=(steps,),
        in_specs=[
            pl.BlockSpec((rows, width), whole),
            pl.BlockSpec((rows, CHUNK), lambda k: (0, k)),
            pl.BlockSpec((rows, width), whole),
            pl.BlockSpec(inverse_deviation.shape, whole),
            pl.BlockSpec((1, width), whole),
            pl.BlockSpec((width, CHUNK), lambda k: (0, k)),
            pl.BlockSpec((width, CHUNK), lambda k: (0, k + steps)),
        ],
        out_specs=[pl.BlockSpec((rows, width), whole), pl.BlockSpec((1, width), whole)],
        out_shape=[
            jax.ShapeDtypeStruct((rows, width), jnp.bfloat16),
            jax.ShapeDtypeStruct((1, width), jnp.float32),
        ],
        scratch_shapes=[pltpu.VMEM((rows, width), jnp.float32)],
        cost_estimate=pl.CostEstimate(
            flops=4 * rows * width * weights.shape[1] // 2,
            transcendentals=0,
            bytes_accessed=2 * weights.size + 2 * rows * weights.shape[1] + 12 * rows * width,
        ),
    )(grad_in, slope, standardized, inverse_deviation, gain_row, weights, weights)


def on_device(x_saved, gains, w_in, w_out, cotangent, lengths):
    rows = cotangent.shape[0]
    width = cotangent.shape[1]
    ends = jnp.cumsum(lengths)
    position = lax.axis_index(DP) * rows + jnp.arange(rows, dtype=jnp.int32)
    utter_hit = (position[:, None] >= ends[None, :]).astype(jnp.int32)
    utter = jnp.sum(utter_hit, 1)
    onehot = (utter[:, None] == jnp.arange(lengths.shape[0], dtype=jnp.int32)[None, :]).astype(
        jnp.int32
    )
    tok_len = jnp.sum(onehot * lengths[None, :], 1).astype(jnp.float32)
    weight = 2.0 * rows / (tok_len + rows)
    current = (cotangent.astype(jnp.float32) * weight[:, None]).astype(jnp.bfloat16)
    xf = x_saved[0].astype(jnp.float32)
    centered_input = xf - jnp.mean(xf, -1, keepdims=True)
    variance = jnp.mean(centered_input * centered_input, -1, keepdims=True)
    inverse_deviation = lax.rsqrt(variance + 1e-05)
    standardized_input = centered_input * inverse_deviation
    gain_vector = gains[0]
    normalized_input = (standardized_input * gain_vector).astype(jnp.bfloat16)
    local = jnp.concatenate([w_in[0], w_out[0].T], axis=1)
    weights = lax.all_gather(local, DP, axis=0, tiled=True)

    inverse_rows = jnp.broadcast_to(inverse_deviation, (rows, 128))
    gain_row = gain_vector[None, :]
    segments = lax.axis_size("segment")
    my_segment = lax.axis_index("segment")
    first = segments - 1
    slope = lax.cond(
        my_segment == first,
        lambda: jnp.zeros((rows, weights.shape[1] // 2), jnp.bfloat16),
        lambda: hidden_slope(normalized_input, weights),
    )

    def keep(grad_in, kept, kept_gain):
        return kept, kept_gain

    result = current
    gain_local = jnp.zeros((1, width), jnp.float32)
    for level in range(first, -1, -1):
        if level == first:
            def mine(grad_in, kept, kept_gain):
                return fused_back(
                    normalized_input, grad_in, standardized_input, inverse_rows, gain_row, weights
                )
        else:
            def mine(grad_in, kept, kept_gain):
                return segment_back(
                    grad_in, slope, standardized_input, inverse_rows, gain_row, weights
                )
        result, gain_local = lax.cond(
            my_segment == level, mine, keep, current, result, gain_local
        )
        if level > 0:
            current = lax.ppermute(result, "segment", [(level, level - 1)])
    pair_sum = gain_local + lax.ppermute(gain_local, "core", [(0, 1), (1, 0)])
    for step in (1, 2):
        pair_sum = pair_sum + lax.ppermute(pair_sum, "y", [(i, i ^ step) for i in range(4)])
    gain_total = lax.psum(pair_sum, "z")
    return (result[None], gain_total)


def solution(mesh):
    n_seg, n_dp = mesh.devices.shape
    shape = (n_seg, n_dp // 8, 4, 2)
    mesh = Mesh(np.asarray(mesh.devices).reshape(shape), ("segment",) + DP)
    in_specs = (
        P("segment", DP, None),
        P("segment", None),
        P("segment", DP, None),
        P("segment", None, DP),
        P(DP, None),
        P(),
    )
    out_specs = (P("segment", DP, None), P("segment", None))
    return jax.shard_map(
        on_device, mesh=mesh, in_specs=in_specs, out_specs=out_specs, check_vma=False
    )
```

```python
import jax
import jax.numpy as jnp
import numpy as np
from jax import lax
from jax.experimental import pallas as pl
from jax.experimental.pallas import tpu as pltpu
from jax.sharding import Mesh, PartitionSpec as P

DP = ("z", "y", "core")
CHUNK = 768


def act_kernel(z_ref, w1_ref, act_ref):
    hidden = jnp.dot(z_ref[...], w1_ref[...], preferred_element_type=jnp.float32)
    sig = jax.nn.sigmoid(hidden)
    act_ref[...] = (sig + hidden * sig * (1.0 - sig)).astype(act_ref.dtype)


def hidden_slope(normed, weights):
    rows, width = normed.shape
    ff = weights.shape[1] // 2
    return pl.pallas_call(
        act_kernel,
        grid=(ff // CHUNK,),
        in_specs=[
            pl.BlockSpec((rows, width), lambda k: (0, 0)),
            pl.BlockSpec((width, CHUNK), lambda k: (0, k)),
        ],
        out_specs=pl.BlockSpec((rows, CHUNK), lambda k: (0, k)),
        out_shape=jax.ShapeDtypeStruct((rows, ff), jnp.bfloat16),
        cost_estimate=pl.CostEstimate(
            flops=2 * rows * width * ff, transcendentals=rows * ff,
            bytes_accessed=2 * width * ff + 2 * rows * ff + 2 * rows * width,
        ),
    )(normed, weights)


def fused_kernel(z_ref, g_ref, xh_ref, inv_ref, gain_ref, w1_ref, w2_ref, out_ref, gp_ref, acc_ref):
    k = pl.program_id(0)

    @pl.when(k == 0)
    def _():
        acc_ref[...] = jnp.zeros_like(acc_ref)

    w1 = w1_ref[...]
    hidden = jnp.dot(z_ref[...], w1, preferred_element_type=jnp.float32)
    up_grad = jnp.dot(g_ref[...], w2_ref[...], preferred_element_type=jnp.float32)
    sig = jax.nn.sigmoid(hidden)
    hid_grad = (0.5 * up_grad * (sig + hidden * sig * (1.0 - sig))).astype(jnp.bfloat16)
    acc_ref[...] += lax.dot_general(
        hid_grad, w1, (((1,), (1,)), ((), ())), preferred_element_type=jnp.float32
    )

    @pl.when(k == pl.num_programs(0) - 1)
    def _():
        norm_backward(acc_ref, xh_ref, inv_ref, gain_ref, g_ref, out_ref, gp_ref)


def norm_backward(acc_ref, xh_ref, inv_ref, gain_ref, g_ref, out_ref, gp_ref):
    norm_gradient = acc_ref[...]
    standardized = xh_ref[...]
    gp_ref[...] = jnp.sum(norm_gradient * standardized, axis=0, keepdims=True)
    gain_scaled = norm_gradient * gain_ref[...]
    mean_e = jnp.mean(gain_scaled, axis=-1, keepdims=True)
    mean_ex = jnp.mean(gain_scaled * standardized, axis=-1, keepdims=True)
    back = inv_ref[:, 0:1] * (gain_scaled - mean_e - standardized * mean_ex)
    out_ref[...] = (g_ref[...].astype(jnp.float32) + back).astype(out_ref.dtype)


def fused_back(normed, grad_in, standardized, inverse_deviation, gain_row, weights):
    rows, width = normed.shape
    steps = weights.shape[1] // 2 // CHUNK
    whole = lambda k: (0, 0)
    return pl.pallas_call(
        fused_kernel,
        grid=(steps,),
        in_specs=[
            pl.BlockSpec((rows, width), whole),
            pl.BlockSpec((rows, width), whole),
            pl.BlockSpec((rows, width), whole),
            pl.BlockSpec(inverse_deviation.shape, whole),
            pl.BlockSpec((1, width), whole),
            pl.BlockSpec((width, CHUNK), lambda k: (0, k)),
            pl.BlockSpec((width, CHUNK), lambda k: (0, k + steps)),
        ],
        out_specs=[pl.BlockSpec((rows, width), whole), pl.BlockSpec((1, width), whole)],
        out_shape=[
            jax.ShapeDtypeStruct((rows, width), jnp.bfloat16),
            jax.ShapeDtypeStruct((1, width), jnp.float32),
        ],
        scratch_shapes=[pltpu.VMEM((rows, width), jnp.float32)],
        cost_estimate=pl.CostEstimate(
            flops=6 * rows * width * weights.shape[1] // 2,
            transcendentals=rows * weights.shape[1] // 2,
            bytes_accessed=2 * weights.size + 12 * rows * width,
        ),
    )(normed, grad_in, standardized, inverse_deviation, gain_row, weights, weights)


def segment_kernel(g_ref, act_ref, xh_ref, inv_ref, gain_ref, w1_ref, w2_ref, out_ref, gp_ref, acc_ref):
    k = pl.program_id(0)

    @pl.when(k == 0)
    def _():
        acc_ref[...] = jnp.zeros_like(acc_ref)

    up_grad = jnp.dot(g_ref[...], w2_ref[...], preferred_element_type=jnp.float32)
    hid_grad = (0.5 * up_grad * act_ref[...].astype(jnp.float32)).astype(jnp.bfloat16)
    acc_ref[...] += lax.dot_general(
        hid_grad, w1_ref[...], (((1,), (1,)), ((), ())), preferred_element_type=jnp.float32
    )

    @pl.when(k == pl.num_programs(0) - 1)
    def _():
        norm_backward(acc_ref, xh_ref, inv_ref, gain_ref, g_ref, out_ref, gp_ref)


def segment_back(grad_in, slope, standardized, inverse_deviation, gain_row, weights):
    rows, width = grad_in.shape
    steps = weights.shape[1] // 2 // CHUNK
    whole = lambda k: (0, 0)
    return pl.pallas_call(
        segment_kernel,
        grid=(steps,),
        in_specs=[
            pl.BlockSpec((rows, width), whole),
            pl.BlockSpec((rows, CHUNK), lambda k: (0, k)),
            pl.BlockSpec((rows, width), whole),
            pl.BlockSpec(inverse_deviation.shape, whole),
            pl.BlockSpec((1, width), whole),
            pl.BlockSpec((width, CHUNK), lambda k: (0, k)),
            pl.BlockSpec((width, CHUNK), lambda k: (0, k + steps)),
        ],
        out_specs=[pl.BlockSpec((rows, width), whole), pl.BlockSpec((1, width), whole)],
        out_shape=[
            jax.ShapeDtypeStruct((rows, width), jnp.bfloat16),
            jax.ShapeDtypeStruct((1, width), jnp.float32),
        ],
        scratch_shapes=[pltpu.VMEM((rows, width), jnp.float32)],
        cost_estimate=pl.CostEstimate(
            flops=4 * rows * width * weights.shape[1] // 2,
            transcendentals=0,
            bytes_accessed=2 * weights.size + 2 * rows * weights.shape[1] + 12 * rows * width,
        ),
    )(grad_in, slope, standardized, inverse_deviation, gain_row, weights, weights)


def on_device(x_saved, gains, w_in, w_out, cotangent, lengths):
    rows = cotangent.shape[0]
    width = cotangent.shape[1]
    ends = jnp.cumsum(lengths)
    position = lax.axis_index(DP) * rows + jnp.arange(rows, dtype=jnp.int32)
    utter_hit = (position[:, None] >= ends[None, :]).astype(jnp.int32)
    utter = jnp.sum(utter_hit, 1)
    onehot = (utter[:, None] == jnp.arange(lengths.shape[0], dtype=jnp.int32)[None, :]).astype(
        jnp.int32
    )
    tok_len = jnp.sum(onehot * lengths[None, :], 1).astype(jnp.float32)
    weight = 2.0 * rows / (tok_len + rows)
    current = (cotangent.astype(jnp.float32) * weight[:, None]).astype(jnp.bfloat16)
    xf = x_saved[0].astype(jnp.float32)
    centered_input = xf - jnp.mean(xf, -1, keepdims=True)
    variance = jnp.mean(centered_input * centered_input, -1, keepdims=True)
    inverse_deviation = lax.rsqrt(variance + 1e-05)
    standardized_input = centered_input * inverse_deviation
    gain_vector = gains[0]
    normalized_input = (standardized_input * gain_vector).astype(jnp.bfloat16)
    local = jnp.concatenate([w_in[0], w_out[0].T], axis=1)
    weights = lax.all_gather(local, DP, axis=0, tiled=True)

    inverse_rows = jnp.broadcast_to(inverse_deviation, (rows, 128))
    gain_row = gain_vector[None, :]
    segments = lax.axis_size("segment")
    my_segment = lax.axis_index("segment")
    first = segments - 1
    slope = lax.cond(
        my_segment == first,
        lambda: jnp.zeros((rows, weights.shape[1] // 2), jnp.bfloat16),
        lambda: hidden_slope(normalized_input, weights),
    )

    def keep(grad_in, kept, kept_gain):
        return kept, kept_gain

    result = current
    gain_local = jnp.zeros((1, width), jnp.float32)
    for level in range(first, -1, -1):
        if level == first:
            def mine(grad_in, kept, kept_gain):
                return fused_back(
                    normalized_input, grad_in, standardized_input, inverse_rows, gain_row, weights
                )
        else:
            def mine(grad_in, kept, kept_gain):
                return segment_back(
                    grad_in, slope, standardized_input, inverse_rows, gain_row, weights
                )
        result, gain_local = lax.cond(
            my_segment == level, mine, keep, current, result, gain_local
        )
        if level > 0:
            current = lax.ppermute(result, "segment", [(level, level - 1)])
    pair_sum = gain_local + lax.ppermute(gain_local, "core", [(0, 1), (1, 0)])
    for step in (1, 2):
        pair_sum = pair_sum + lax.ppermute(pair_sum, "y", [(i, i ^ step) for i in range(4)])
    for step in (1, 2, 4):
        pair_sum = pair_sum + lax.ppermute(pair_sum, "z", [(i, i ^ step) for i in range(8)])
    gain_total = pair_sum
    return (result[None], gain_total)


def solution(mesh):
    n_seg, n_dp = mesh.devices.shape
    shape = (n_seg, n_dp // 8, 4, 2)
    mesh = Mesh(np.asarray(mesh.devices).reshape(shape), ("segment",) + DP)
    in_specs = (
        P("segment", DP, None),
        P("segment", None),
        P("segment", DP, None),
        P("segment", None, DP),
        P(DP, None),
        P(),
    )
    out_specs = (P("segment", DP, None), P("segment", None))
    return jax.shard_map(
        on_device, mesh=mesh, in_specs=in_specs, out_specs=out_specs, check_vma=False
    )
```
